128 devices in a mesh: gx: 16 (over z, x), gy: 8 (over y, core).
Axes of the slice: x: 4, y: 4, z: 4, core: 2. Of those that a mesh axis runs over, the one named last changes fastest.
Arguments:
- field: float32 [64, 128, 16, 384], P('gx', 'gy'), may hold values from -6 to 6
- inv_material: float32 [64, 128, 16], P('gx', 'gy'), may hold values from 0.5 to 2
- stiffness: bfloat16 [384, 384], replicated, may hold values from -0.15625 to 0.15625
- lift: bfloat16 [576, 384], replicated, may hold values from -1.25 to 1.25
- projection: bfloat16 [96, 64], replicated, may hold values from -0.625 to 0.625
- back_lift: bfloat16 [64, 384], replicated, may hold values from -0.75 to 0.75
- op_blocks: bfloat16 [8, 4, 64, 64], replicated, may hold values from -0.375 to 0.375
- op_columns: int32 [8, 4], replicated, may hold values from 0 to 7
- panel_dest: int32 [8192, 1], P(('gx', 'gy')), may hold values from 0 to 127; in each aligned block of 64 rows (0 to 63, 64 to 127, ...) at most 2 rows name the same one
- panel_anchor: int32 [8192], P(('gx', 'gy')), may hold values from 0 to 7
Outputs:
- advanced: float32 [64, 128, 16, 384], P('gx', 'gy')
The draws below stay inside these ranges and needn't reach their ends.
Inputs may be any that keep to these rules, and one draw needn't show every extreme that they name: `panel_dest`: among the 64 panels of one device no brick is named more than 2 times; some device names one brick exactly 2 times.
All inputs are finite; a program needn't handle non-finite values.
Results may differ from the reference program's by a relative error of at most 0.0084.
Values may be sent and summed in bfloat16 or wider, within the bound.
No kernel may reach another device: no remote copies, remote signals or barrier semaphores. Data moves between devices by JAX's collectives and lax.ppermute only.
A program may use at most 128 MiB of HBM per device.

```python
import math
import jax
import jax.numpy as jnp
import numpy as np
from jax import lax

EX = 4
EY = 16
EZ = 16
NBLK = 8
KB = 4
NXE = 64
NYE = 128
PAN_DEV = 64
PANELS = 8192
CAP = 2
N_GX = 16
N_GY = 8
DEVICES = 128


def place_ends(array, stream_key, smallest, largest):
    place = [jax.random.randint(jax.random.fold_in(stream_key, axis), (), 0, length) for axis, length in enumerate(array.shape)]
    longest = array.shape.index(max(array.shape))
    next_to = place[:longest] + [(place[longest] + 1) % array.shape[longest]] + place[longest + 1:]
    return array.at[tuple(place)].set(smallest).at[tuple(next_to)].set(largest)


def levels(key, dims, shards, low, largest):
    def one(axis_at, blocks):
        steps = jax.random.uniform(jax.random.fold_in(jax.random.fold_in(key, 6), axis_at), (blocks,), jnp.float32, low / len(shards), largest / len(shards))
        return jnp.repeat(jnp.exp(steps), dims[axis_at] // blocks).reshape((-1,) + (1,) * (len(dims) - axis_at - 1))

    factor_of = one(*shards[0])
    for cut in shards[1:]:
        factor_of = factor_of * one(*cut)
    return factor_of


def routed_block(stream_key, own, number, rows, count, top, reach, slope):
    sequence = jax.random.permutation(stream_key, count)
    packed, common = load_shares(count, rows * top, reach, slope, True), load_shares(count, rows * top, reach, slope, False)
    places = jnp.arange(count)

    def named(sizes, rotation):
        used = int((sizes > 0).sum())
        fixed = max(1, used // 4)
        shifted = fixed + (places - fixed + rotation * (used - fixed)) % max(1, count - fixed)
        return jnp.zeros((count,), jnp.int32).at[sequence[jnp.where(places < fixed, places, shifted)]].set(jnp.asarray(sizes, jnp.int32))

    sizes = jnp.where(number % 4 == 0, named(packed, number // 4), named(common, number - number // 4 - 1))
    mixed = jax.random.permutation(jax.random.fold_in(own, 3), count)
    donor, taker = mixed[0:count // 2 * 2:2], mixed[1:count // 2 * 2:2]
    margin = jnp.minimum(sizes[donor] - 1, reach - sizes[taker]) // 2
    margin = jnp.where((donor == sequence[0]) | (taker == sequence[0]) | (sizes[taker] == 0), 0, jnp.maximum(margin, 0))
    shifted = jax.random.randint(jax.random.fold_in(own, 4), (count // 2,), 0, 1 << 20) % (margin + 1)
    sizes = sizes.at[donor].add(-shifted).at[taker].add(shifted)
    items = jnp.searchsorted(jnp.cumsum(sizes), jnp.arange(rows * top), side="right").astype(jnp.int32)
    listing = items.reshape(top, rows).T
    listing = listing[jax.random.permutation(jax.random.fold_in(own, 1), rows)]
    rotation = jax.random.randint(jax.random.fold_in(own, 2), (rows, 1), 0, top)
    return jnp.take_along_axis(listing, (jnp.arange(top)[None, :] + rotation) % top, axis=1)


def load_shares(amount, total, reach, slope, full):
    portions = [(1 << 20) // math.isqrt(grade ** slope) + 1 for grade in range(1, amount + 1)]
    largest = reach if full else min(reach, max(-(-total // amount), total * portions[0] // sum(portions)))
    least = 1 if total - largest >= amount - 1 else 0
    given, surplus = [largest] + [least] * (amount - 1), total - largest - least * (amount - 1)
    while surplus > 0:
        candidates = [i for i in range(1, amount) if given[i] < largest] or [i for i in range(1, amount) if given[i] < reach]
        mass, budget = sum([portions[i] for i in candidates]), surplus
        for i in candidates:
            more = min(reach - given[i], max(1, budget * portions[i] // mass), surplus)
            given[i] = given[i] + more
            surplus = surplus - more
    return np.array(given)


def centred(key, extent, deviation, reach, cuts=(), held_as=jnp.bfloat16):
    level = levels(key, extent, cuts, -0.22, 0.18) if cuts else 1.0
    drawn = jax.random.normal(key, extent, jnp.float32) * deviation * level
    return jnp.minimum(jnp.maximum(drawn, -reach), reach).astype(held_as)


def setup_inputs(seed: int = 0) -> dict:
    seeds = jax.random.split(jax.random.key(seed), 11)
    field = centred(seeds[0], (NXE, NYE, EZ, 384), 1.0, 6.0, ((0, 16), (1, 8)), jnp.float32)
    inv_material = jnp.clip(jnp.exp(math.log(2.0) - 1.3862944 * jax.random.uniform(seeds[1], (NXE, NYE, EZ), jnp.float32) ** levels(seeds[1], (NXE, NYE, EZ), ((0, 16), (1, 8)), -0.2, 0.2)), 0.5, 2.0)
    stiffness = centred(seeds[2], (384, 384), 1536 ** -0.5, 0.15625)
    lift = centred(seeds[3], (576, 384), 24 ** -0.5, 1.25)
    projection = centred(seeds[4], (96, 64), 96 ** -0.5, 0.625)
    back_lift = centred(seeds[5], (64, 384), 64 ** -0.5, 0.75)
    op_blocks = centred(seeds[6], (NBLK, KB, 64, 64), 256 ** -0.5, 0.375)
    op_columns = place_ends(jax.random.randint(seeds[7], (NBLK, KB), 0, NBLK), jax.random.fold_in(seeds[7], 1), 0, NBLK - 1).astype(jnp.int32)
    panel_dest_keys = jax.random.split(jax.random.fold_in(seeds[8], 1), PANELS // PAN_DEV)
    panel_dest_turns = jax.random.permutation(jax.random.fold_in(seeds[8], 3), PANELS // PAN_DEV)
    panel_dest = jax.vmap(lambda own, number: routed_block(jax.random.fold_in(seeds[8], 2), own, number, PAN_DEV, DEVICES, 1, CAP, 2))(panel_dest_keys, panel_dest_turns).reshape((PANELS, 1))
    panel_anchor = place_ends(jax.random.randint(seeds[9], (PANELS,), 0, NBLK), jax.random.fold_in(seeds[9], 1), 0, NBLK - 1).astype(jnp.int32)
    return dict(field=field, inv_material=inv_material, stiffness=stiffness, lift=lift, projection=projection, back_lift=back_lift, op_blocks=op_blocks, op_columns=op_columns, panel_dest=panel_dest, panel_anchor=panel_anchor)


step_size = 0.25


def face_traces(tr):
    lead = tr.shape[:3]
    shape = lead + (96,)
    return (tr[..., 0, :, :].reshape(shape), tr[..., 3, :, :].reshape(shape),
            tr[..., :, 0, :].reshape(shape), tr[..., :, 3, :].reshape(shape),
            tr[..., 0].reshape(shape), tr[..., 3].reshape(shape))


def lower_of(arr, axis):
    size = arr.shape[axis]
    zero = jnp.zeros_like(lax.slice_in_dim(arr, 0, 1, axis=axis))
    return jnp.concatenate([zero, lax.slice_in_dim(arr, 0, size - 1, axis=axis)], axis)


def upper_of(arr, axis):
    size = arr.shape[axis]
    zero = jnp.zeros_like(lax.slice_in_dim(arr, 0, 1, axis=axis))
    return jnp.concatenate([lax.slice_in_dim(arr, 1, size, axis=axis), zero], axis)


def rate(section, inv_material, stiffness, lift, projection, back_lift, op_blocks, op_columns, dest, anchor):
    nxe, nye, nze = section.shape[:3]
    devices = N_GX * N_GY
    sb = section.astype(jnp.bfloat16)
    tr = sb.reshape((nxe, nye, nze, 6, 4, 4, 4))
    xlo, xhi, ylo, yhi, zlo, zhi = face_traces(tr)
    f32 = jnp.float32
    jumps = jnp.concatenate([
        lower_of(xhi, 0).astype(f32) - xlo.astype(f32), upper_of(xlo, 0).astype(f32) - xhi.astype(f32),
        lower_of(yhi, 1).astype(f32) - ylo.astype(f32), upper_of(ylo, 1).astype(f32) - yhi.astype(f32),
        lower_of(zhi, 2).astype(f32) - zlo.astype(f32), upper_of(zlo, 2).astype(f32) - zhi.astype(f32)], -1).astype(jnp.bfloat16)
    volume = jnp.dot(sb.reshape(-1, 384), stiffness, preferred_element_type=f32)
    faces = jnp.dot(jumps.reshape(-1, 576), lift, preferred_element_type=f32)
    total = (volume + faces).reshape(nxe, nye, nze, 384)
    tops = zhi[:, :, nze - 1, :]
    tops = tops.reshape(N_GX, EX, N_GY, EY, 96).transpose(0, 2, 1, 3, 4).reshape(-1, 96)
    u = jnp.dot(tops, projection, preferred_element_type=f32).astype(jnp.bfloat16)
    ids = (dest * NBLK + anchor).astype(jnp.int32)
    grid = jax.ops.segment_sum(u.astype(f32), ids, num_segments=devices * NBLK)
    grid = grid.reshape(devices, NBLK, 64).astype(jnp.bfloat16)
    gsel = grid[:, op_columns]
    w = jnp.einsum('dikc,ikce->die', gsel.astype(f32), op_blocks.astype(f32)).astype(jnp.bfloat16)
    v = w.reshape(devices * NBLK, 64)[ids]
    bvals = jnp.dot(v, back_lift, preferred_element_type=f32)
    bvals = bvals.reshape(N_GX, N_GY, EX, EY, 384).transpose(0, 2, 1, 3, 4).reshape(nxe, nye, 384)
    total = total.at[:, :, nze - 1, :].add(bvals)
    return inv_material[..., None] * total


def reference(field, inv_material, stiffness, lift, projection, back_lift, op_blocks, op_columns, panel_dest, panel_anchor):
    dest = panel_dest[:, 0]

    def evaluate(section):
        return rate(section, inv_material, stiffness, lift, projection, back_lift, op_blocks, op_columns, dest, panel_anchor)

    k_one = evaluate(field)
    k_two = evaluate(field + (step_size / 2) * k_one)
    k_three = evaluate(field + (step_size / 2) * k_two)
    k_four = evaluate(field + step_size * k_three)
    return field + (step_size / 6) * (k_one + 2.0 * k_two + 2.0 * k_three + k_four)
```

```python
import jax
import jax.numpy as jnp
from jax import lax
from jax.sharding import PartitionSpec as P

NBLK = 8
LANE = 128

step_size = 0.25


def shift_in(arr, axis, dim, lower):
    count = lax.axis_size(axis)
    if lower:
        pairs = [(i, i + 1) for i in range(count - 1)]
    else:
        pairs = [(i + 1, i) for i in range(count - 1)]
    return lax.ppermute(arr, axis, pairs)


def trace_selector():
    rows = lax.broadcasted_iota(jnp.int32, (384, 6 * LANE), 0)
    cols = lax.broadcasted_iota(jnp.int32, (384, 6 * LANE), 1)
    face, j = cols // LANE, cols % LANE
    comp, p, q = j // 16, (j // 4) % 4, j % 4
    side = jnp.where(face % 2 == 0, 0, 3)
    ax = face // 2
    a = jnp.where(ax == 0, side, p)
    b = jnp.where(ax == 0, p, jnp.where(ax == 1, side, q))
    c = jnp.where(ax == 2, side, q)
    src = comp * 64 + a * 16 + b * 4 + c
    return ((rows == src) & (j < 96)).astype(jnp.bfloat16)


def pad_faces(mat):
    k = mat.shape[1]
    zero = jnp.zeros((LANE - 96, k), mat.dtype)
    parts = []
    for f in range(6):
        parts += [mat[96 * f:96 * (f + 1)], zero]
    return jnp.concatenate(parts, 0)


def boundary_term(tops, proj_pad, back_lift, op_blocks, op_columns, place, recv_onehot, devices, capacity):
    f32 = jnp.float32
    u = jnp.dot(tops, proj_pad, preferred_element_type=f32).astype(jnp.bfloat16)
    send_u = jnp.einsum("pr,pc->rc", place, u, preferred_element_type=f32).astype(jnp.bfloat16)
    recv_u = lax.all_to_all(send_u.reshape(devices, capacity, 64), ("gx", "gy"), 0, 0, tiled=True)
    recv_u = recv_u.reshape(devices * capacity, 64)
    grid = jnp.einsum("rb,rc->bc", recv_onehot, recv_u, preferred_element_type=f32).astype(jnp.bfloat16)
    select = (op_columns[:, :, None] == jnp.arange(NBLK, dtype=jnp.int32)[None, None, :]).astype(jnp.bfloat16)
    gsel = jnp.einsum("ikj,jc->ikc", select, grid, preferred_element_type=f32).astype(jnp.bfloat16)
    w = jnp.einsum("ikc,ikce->ie", gsel, op_blocks, preferred_element_type=f32).astype(jnp.bfloat16)
    reply = jnp.dot(recv_onehot, w, preferred_element_type=f32).astype(jnp.bfloat16)
    back = lax.all_to_all(reply.reshape(devices, capacity, 64), ("gx", "gy"), 0, 0, tiled=True)
    back = back.reshape(devices * capacity, 64)
    values = jnp.dot(place, back, preferred_element_type=f32).astype(jnp.bfloat16)
    return jnp.dot(values, back_lift, preferred_element_type=f32)


def body(field, inv_material, stiffness, lift, projection, back_lift, op_blocks, op_columns, panel_dest, panel_anchor):
    f32, bf16 = jnp.float32, jnp.bfloat16
    ex_n, ey_n, ez_n = field.shape[:3]
    n = ex_n * ey_n * ez_n
    devices = lax.axis_size("gx") * lax.axis_size("gy")
    panels = ex_n * ey_n
    capacity = max(2, 2 * panels // devices)
    dest = panel_dest[:, 0]
    hit = (dest[:, None] == jnp.arange(devices, dtype=jnp.int32)[None, :]).astype(jnp.int32)
    ranks = jnp.cumsum(hit, axis=0)
    slots = jnp.sum(hit * (ranks - 1), axis=1)
    position = dest * capacity + slots
    place = (position[:, None] == jnp.arange(devices * capacity, dtype=jnp.int32)[None, :]).astype(bf16)
    code = jnp.einsum("pr,p->r", place, (panel_anchor + 1).astype(bf16), preferred_element_type=f32).astype(bf16)
    recv_code = lax.all_to_all(code.reshape(devices, capacity), ("gx", "gy"), 0, 0, tiled=True)
    recv_code = recv_code.reshape(devices * capacity)
    levels = (jnp.arange(NBLK, dtype=jnp.int32) + 1).astype(bf16)
    recv_onehot = (recv_code[:, None] == levels[None, :]).astype(bf16)

    sel = trace_selector()
    lift_pad = pad_faces(lift)
    proj_pad = jnp.concatenate([projection, jnp.zeros((LANE - 96, 64), bf16)], 0)
    inv = inv_material.reshape(n, 1)
    zero_z = jnp.zeros((ex_n, ey_n, 1, LANE), bf16)

    def evaluate(section):
        sb = section.reshape(n, 384).astype(bf16)
        t = jnp.dot(sb, sel, preferred_element_type=f32).astype(bf16)
        t4 = t.reshape(ex_n, ey_n, ez_n, 6 * LANE)
        xlo, xhi = t4[..., 0:LANE], t4[..., LANE:2 * LANE]
        ylo, yhi = t4[..., 2 * LANE:3 * LANE], t4[..., 3 * LANE:4 * LANE]
        zlo, zhi = t4[..., 4 * LANE:5 * LANE], t4[..., 5 * LANE:6 * LANE]
        halo_xl = shift_in(xhi[ex_n - 1:], "gx", 0, True)
        halo_xr = shift_in(xlo[:1], "gx", 0, False)
        halo_yl = shift_in(yhi[:, ey_n - 1:], "gy", 1, True)
        halo_yr = shift_in(ylo[:, :1], "gy", 1, False)
        tops = zhi[:, :, ez_n - 1, :].reshape(panels, LANE)
        bvals = boundary_term(tops, proj_pad, back_lift, op_blocks, op_columns, place, recv_onehot, devices, capacity)
        nb = jnp.concatenate([
            jnp.concatenate([halo_xl, xhi[:ex_n - 1]], 0),
            jnp.concatenate([xlo[1:], halo_xr], 0),
            jnp.concatenate([halo_yl, yhi[:, :ey_n - 1]], 1),
            jnp.concatenate([ylo[:, 1:], halo_yr], 1),
            jnp.concatenate([zero_z, zhi[:, :, :ez_n - 1]], 2),
            jnp.concatenate([zlo[:, :, 1:], zero_z], 2),
        ], -1)
        jumps = (nb.astype(f32) - t4.astype(f32)).astype(bf16).reshape(n, 6 * LANE)
        volume = jnp.dot(sb, stiffness, preferred_element_type=f32)
        faces = jnp.dot(jumps, lift_pad, preferred_element_type=f32)
        total = (volume + faces).reshape(ex_n, ey_n, ez_n, 384)
        total = total.at[:, :, ez_n - 1, :].add(bvals.reshape(ex_n, ey_n, 384))
        return inv_material[..., None] * total

    k_one = evaluate(field)
    k_two = evaluate(field + step_size / 2 * k_one)
    k_three = evaluate(field + step_size / 2 * k_two)
    k_four = evaluate(field + step_size * k_three)
    return field + step_size / 6 * (k_one + 2.0 * k_two + 2.0 * k_three + k_four)


def solution(mesh):
    return jax.shard_map(
        body,
        mesh=mesh,
        in_specs=(
            P("gx", "gy", None, None),
            P("gx", "gy", None),
            P(), P(), P(), P(), P(), P(),
            P(("gx", "gy"), None),
            P(("gx", "gy")),
        ),
        out_specs=P("gx", "gy", None, None),
        check_vma=False,
    )
```

```python
import jax
import jax.numpy as jnp
from jax import lax
from jax.sharding import PartitionSpec as P
from jax.experimental import pallas as pl
from jax.experimental.pallas import tpu as pltpu
import functools

NBLK = 8
LANE = 128

step_size = 0.25


def rate_kernel(ex_n, ey_n, ez_n, sb_ref, t_ref, xl_ref, xr_ref, yl_ref, yr_ref, stiff_ref, lift_ref, out_ref):
    f32, bf16 = jnp.float32, jnp.bfloat16
    n = ex_n * ey_n * ez_n
    plane = ey_n * ez_n
    row = lax.broadcasted_iota(jnp.int32, (n, LANE), 0)
    ez = row % ez_n
    parts = []
    own = t_ref[:, 0:LANE].astype(f32)
    nb = jnp.concatenate([xl_ref[...], t_ref[0:n - plane, LANE:2 * LANE]], 0).astype(f32)
    parts.append((nb - own).astype(bf16))
    own = t_ref[:, LANE:2 * LANE].astype(f32)
    nb = jnp.concatenate([t_ref[plane:n, 0:LANE], xr_ref[...]], 0).astype(f32)
    parts.append((nb - own).astype(bf16))
    own = t_ref[:, 2 * LANE:3 * LANE].astype(f32)
    pieces = []
    for ex in range(ex_n):
        pieces.append(yl_ref[ex * ez_n:(ex + 1) * ez_n, :])
        pieces.append(t_ref[ex * plane:(ex + 1) * plane - ez_n, 3 * LANE:4 * LANE])
    nb = jnp.concatenate(pieces, 0).astype(f32)
    parts.append((nb - own).astype(bf16))
    own = t_ref[:, 3 * LANE:4 * LANE].astype(f32)
    pieces = []
    for ex in range(ex_n):
        pieces.append(t_ref[ex * plane + ez_n:(ex + 1) * plane, 2 * LANE:3 * LANE])
        pieces.append(yr_ref[ex * ez_n:(ex + 1) * ez_n, :])
    nb = jnp.concatenate(pieces, 0).astype(f32)
    parts.append((nb - own).astype(bf16))
    zlo = t_ref[:, 4 * LANE:5 * LANE].astype(f32)
    zhi = t_ref[:, 5 * LANE:6 * LANE].astype(f32)
    nb = jnp.where(ez == 0, 0.0, pltpu.roll(zhi, 1, 0))
    parts.append((nb - zlo).astype(bf16))
    nb = jnp.where(ez == ez_n - 1, 0.0, pltpu.roll(zlo, n - 1, 0))
    parts.append((nb - zhi).astype(bf16))
    jumps = jnp.concatenate(parts, -1)
    out_ref[...] = (jnp.dot(sb_ref[...], stiff_ref[...], preferred_element_type=f32)
                    + jnp.dot(jumps, lift_ref[...], preferred_element_type=f32))


def rate_call(sb, t, xl, xr, yl, yr, stiff, lift_pad, dims):
    ex_n, ey_n, ez_n = dims
    n = ex_n * ey_n * ez_n
    vm = pl.BlockSpec(memory_space=pltpu.VMEM)
    flops = 2 * n * 384 * (384 + 6 * LANE)
    return pl.pallas_call(
        functools.partial(rate_kernel, ex_n, ey_n, ez_n),
        out_shape=jax.ShapeDtypeStruct((n, 384), jnp.float32),
        in_specs=[vm] * 8,
        out_specs=vm,
        cost_estimate=pl.CostEstimate(flops=flops, bytes_accessed=n * (384 * 2 + 768 * 2 + 384 * 4), transcendentals=0),
    )(sb, t, xl, xr, yl, yr, stiff, lift_pad)


def shift_in(arr, axis, dim, lower):
    count = lax.axis_size(axis)
    if lower:
        pairs = [(i, i + 1) for i in range(count - 1)]
    else:
        pairs = [(i + 1, i) for i in range(count - 1)]
    return lax.ppermute(arr, axis, pairs)


def trace_selector():
    rows = lax.broadcasted_iota(jnp.int32, (384, 6 * LANE), 0)
    cols = lax.broadcasted_iota(jnp.int32, (384, 6 * LANE), 1)
    face, j = cols // LANE, cols % LANE
    comp, p, q = j // 16, (j // 4) % 4, j % 4
    side = jnp.where(face % 2 == 0, 0, 3)
    ax = face // 2
    a = jnp.where(ax == 0, side, p)
    b = jnp.where(ax == 0, p, jnp.where(ax == 1, side, q))
    c = jnp.where(ax == 2, side, q)
    src = comp * 64 + a * 16 + b * 4 + c
    return ((rows == src) & (j < 96)).astype(jnp.bfloat16)


def pad_faces(mat):
    k = mat.shape[1]
    zero = jnp.zeros((LANE - 96, k), mat.dtype)
    parts = []
    for f in range(6):
        parts += [mat[96 * f:96 * (f + 1)], zero]
    return jnp.concatenate(parts, 0)


def boundary_term(tops, proj_pad, back_lift, op_blocks, op_columns, place, recv_onehot, devices, capacity):
    f32 = jnp.float32
    u = jnp.dot(tops, proj_pad, preferred_element_type=f32).astype(jnp.bfloat16)
    send_u = jnp.einsum("pr,pc->rc", place, u, preferred_element_type=f32).astype(jnp.bfloat16)
    recv_u = lax.all_to_all(send_u.reshape(devices, capacity, 64), ("gx", "gy"), 0, 0, tiled=True)
    recv_u = recv_u.reshape(devices * capacity, 64)
    grid = jnp.einsum("rb,rc->bc", recv_onehot, recv_u, preferred_element_type=f32).astype(jnp.bfloat16)
    select = (op_columns[:, :, None] == jnp.arange(NBLK, dtype=jnp.int32)[None, None, :]).astype(jnp.bfloat16)
    gsel = jnp.einsum("ikj,jc->ikc", select, grid, preferred_element_type=f32).astype(jnp.bfloat16)
    w = jnp.einsum("ikc,ikce->ie", gsel, op_blocks, preferred_element_type=f32).astype(jnp.bfloat16)
    reply = jnp.dot(recv_onehot, w, preferred_element_type=f32).astype(jnp.bfloat16)
    back = lax.all_to_all(reply.reshape(devices, capacity, 64), ("gx", "gy"), 0, 0, tiled=True)
    back = back.reshape(devices * capacity, 64)
    values = jnp.dot(place, back, preferred_element_type=f32).astype(jnp.bfloat16)
    return jnp.dot(values, back_lift, preferred_element_type=f32)


def body(field, inv_material, stiffness, lift, projection, back_lift, op_blocks, op_columns, panel_dest, panel_anchor):
    f32, bf16 = jnp.float32, jnp.bfloat16
    ex_n, ey_n, ez_n = field.shape[:3]
    n = ex_n * ey_n * ez_n
    devices = lax.axis_size("gx") * lax.axis_size("gy")
    panels = ex_n * ey_n
    capacity = max(2, 2 * panels // devices)
    dest = panel_dest[:, 0]
    hit = (dest[:, None] == jnp.arange(devices, dtype=jnp.int32)[None, :]).astype(jnp.int32)
    ranks = jnp.cumsum(hit, axis=0)
    slots = jnp.sum(hit * (ranks - 1), axis=1)
    position = dest * capacity + slots
    place = (position[:, None] == jnp.arange(devices * capacity, dtype=jnp.int32)[None, :]).astype(bf16)
    code = jnp.einsum("pr,p->r", place, (panel_anchor + 1).astype(bf16), preferred_element_type=f32).astype(bf16)
    recv_code = lax.all_to_all(code.reshape(devices, capacity), ("gx", "gy"), 0, 0, tiled=True)
    recv_code = recv_code.reshape(devices * capacity)
    levels = (jnp.arange(NBLK, dtype=jnp.int32) + 1).astype(bf16)
    recv_onehot = (recv_code[:, None] == levels[None, :]).astype(bf16)

    sel = trace_selector()
    lift_pad = pad_faces(lift)
    proj_pad = jnp.concatenate([projection, jnp.zeros((LANE - 96, 64), bf16)], 0)
    inv = inv_material.reshape(n, 1)
    zero_z = jnp.zeros((ex_n, ey_n, 1, LANE), bf16)

    def evaluate(section):
        sb = section.reshape(n, 384).astype(bf16)
        t = jnp.dot(sb, sel, preferred_element_type=f32).astype(bf16)
        t4 = t.reshape(ex_n, ey_n, ez_n, 6 * LANE)
        xlo, xhi = t4[..., 0:LANE], t4[..., LANE:2 * LANE]
        ylo, yhi = t4[..., 2 * LANE:3 * LANE], t4[..., 3 * LANE:4 * LANE]
        zlo, zhi = t4[..., 4 * LANE:5 * LANE], t4[..., 5 * LANE:6 * LANE]
        halo_xl = shift_in(xhi[ex_n - 1:], "gx", 0, True)
        halo_xr = shift_in(xlo[:1], "gx", 0, False)
        halo_yl = shift_in(yhi[:, ey_n - 1:], "gy", 1, True)
        halo_yr = shift_in(ylo[:, :1], "gy", 1, False)
        tops = zhi[:, :, ez_n - 1, :].reshape(panels, LANE)
        bvals = boundary_term(tops, proj_pad, back_lift, op_blocks, op_columns, place, recv_onehot, devices, capacity)
        total = rate_call(
            sb, t,
            halo_xl.reshape(ey_n * ez_n, LANE), halo_xr.reshape(ey_n * ez_n, LANE),
            halo_yl.reshape(ex_n * ez_n, LANE), halo_yr.reshape(ex_n * ez_n, LANE),
            stiffness, lift_pad, (ex_n, ey_n, ez_n),
        ).reshape(ex_n, ey_n, ez_n, 384)
        top = total[:, :, ez_n - 1:, :] + bvals.reshape(ex_n, ey_n, 1, 384)
        total = jnp.concatenate([total[:, :, :ez_n - 1, :], top], 2)
        return inv_material[..., None] * total

    k_one = evaluate(field)
    k_two = evaluate(field + step_size / 2 * k_one)
    k_three = evaluate(field + step_size / 2 * k_two)
    k_four = evaluate(field + step_size * k_three)
    return field + step_size / 6 * (k_one + 2.0 * k_two + 2.0 * k_three + k_four)


def solution(mesh):
    return jax.shard_map(
        body,
        mesh=mesh,
        in_specs=(
            P("gx", "gy", None, None),
            P("gx", "gy", None),
            P(), P(), P(), P(), P(), P(),
            P(("gx", "gy"), None),
            P(("gx", "gy")),
        ),
        out_specs=P("gx", "gy", None, None),
        check_vma=False,
    )
```

```python
import jax
import jax.numpy as jnp
from jax import lax
from jax.sharding import PartitionSpec as P
from jax.experimental import pallas as pl
from jax.experimental.pallas import tpu as pltpu
import functools

NBLK = 8
LANE = 128

step_size = 0.25


def rate_kernel(ex_n, ey_n, ez_n, sb_ref, t_ref, xl_ref, xr_ref, yl_ref, yr_ref, stiff_ref, lift_ref, out_ref):
    f32, bf16 = jnp.float32, jnp.bfloat16
    n = ex_n * ey_n * ez_n
    plane = ey_n * ez_n
    row = lax.broadcasted_iota(jnp.int32, (n, LANE), 0)
    ez = row % ez_n
    parts = []
    own = t_ref[:, 0:LANE].astype(f32)
    nb = jnp.concatenate([xl_ref[...], t_ref[0:n - plane, LANE:2 * LANE]], 0).astype(f32)
    parts.append((nb - own).astype(bf16))
    own = t_ref[:, LANE:2 * LANE].astype(f32)
    nb = jnp.concatenate([t_ref[plane:n, 0:LANE], xr_ref[...]], 0).astype(f32)
    parts.append((nb - own).astype(bf16))
    own = t_ref[:, 2 * LANE:3 * LANE].astype(f32)
    pieces = []
    for ex in range(ex_n):
        pieces.append(yl_ref[ex * ez_n:(ex + 1) * ez_n, :])
        pieces.append(t_ref[ex * plane:(ex + 1) * plane - ez_n, 3 * LANE:4 * LANE])
    nb = jnp.concatenate(pieces, 0).astype(f32)
    parts.append((nb - own).astype(bf16))
    own = t_ref[:, 3 * LANE:4 * LANE].astype(f32)
    pieces = []
    for ex in range(ex_n):
        pieces.append(t_ref[ex * plane + ez_n:(ex + 1) * plane, 2 * LANE:3 * LANE])
        pieces.append(yr_ref[ex * ez_n:(ex + 1) * ez_n, :])
    nb = jnp.concatenate(pieces, 0).astype(f32)
    parts.append((nb - own).astype(bf16))
    zlo = t_ref[:, 4 * LANE:5 * LANE].astype(f32)
    zhi = t_ref[:, 5 * LANE:6 * LANE].astype(f32)
    nb = jnp.where(ez == 0, 0.0, pltpu.roll(zhi, 1, 0))
    parts.append((nb - zlo).astype(bf16))
    nb = jnp.where(ez == ez_n - 1, 0.0, pltpu.roll(zlo, n - 1, 0))
    parts.append((nb - zhi).astype(bf16))
    jumps = jnp.concatenate(parts, -1)
    out_ref[...] = (jnp.dot(sb_ref[...], stiff_ref[...], preferred_element_type=f32)
                    + jnp.dot(jumps, lift_ref[...], preferred_element_type=f32))


def rate_call(sb, t, xl, xr, yl, yr, stiff, lift_pad, dims):
    ex_n, ey_n, ez_n = dims
    n = ex_n * ey_n * ez_n
    vm = pl.BlockSpec(memory_space=pltpu.VMEM)
    flops = 2 * n * 384 * (384 + 6 * LANE)
    return pl.pallas_call(
        functools.partial(rate_kernel, ex_n, ey_n, ez_n),
        out_shape=jax.ShapeDtypeStruct((n, 384), jnp.float32),
        in_specs=[vm] * 8,
        out_specs=vm,
        cost_estimate=pl.CostEstimate(flops=flops, bytes_accessed=n * (384 * 2 + 768 * 2 + 384 * 4), transcendentals=0),
    )(sb, t, xl, xr, yl, yr, stiff, lift_pad)


def shift_in(arr, axis, dim, lower):
    count = lax.axis_size(axis)
    if lower:
        pairs = [(i, i + 1) for i in range(count - 1)]
    else:
        pairs = [(i + 1, i) for i in range(count - 1)]
    return lax.ppermute(arr, axis, pairs)


def trace_selector():
    rows = lax.broadcasted_iota(jnp.int32, (384, 6 * LANE), 0)
    cols = lax.broadcasted_iota(jnp.int32, (384, 6 * LANE), 1)
    face, j = cols // LANE, cols % LANE
    comp, p, q = j // 16, (j // 4) % 4, j % 4
    side = jnp.where(face % 2 == 0, 0, 3)
    ax = face // 2
    a = jnp.where(ax == 0, side, p)
    b = jnp.where(ax == 0, p, jnp.where(ax == 1, side, q))
    c = jnp.where(ax == 2, side, q)
    src = comp * 64 + a * 16 + b * 4 + c
    return ((rows == src) & (j < 96)).astype(jnp.bfloat16)


def pad_faces(mat):
    k = mat.shape[1]
    zero = jnp.zeros((LANE - 96, k), mat.dtype)
    parts = []
    for f in range(6):
        parts += [mat[96 * f:96 * (f + 1)], zero]
    return jnp.concatenate(parts, 0)


def boundary_term(tops, proj_pad, back_lift, op_blocks, op_columns, place, recv_onehot, devices, capacity, halos):
    f32 = jnp.float32
    u = jnp.dot(tops, proj_pad, preferred_element_type=f32).astype(jnp.bfloat16)
    send_u = jnp.einsum("pr,pc->rc", place, u, preferred_element_type=f32).astype(jnp.bfloat16)
    recv_u = lax.all_to_all(send_u.reshape(devices, capacity, 64), ("gx", "gy"), 0, 0, tiled=True)
    recv_u = recv_u.reshape(devices * capacity, 64)
    grid = jnp.einsum("rb,rc->bc", recv_onehot, recv_u, preferred_element_type=f32).astype(jnp.bfloat16)
    select = (op_columns[:, :, None] == jnp.arange(NBLK, dtype=jnp.int32)[None, None, :]).astype(jnp.bfloat16)
    gsel = jnp.einsum("ikj,jc->ikc", select, grid, preferred_element_type=f32).astype(jnp.bfloat16)
    w = jnp.einsum("ikc,ikce->ie", gsel, op_blocks, preferred_element_type=f32).astype(jnp.bfloat16)
    reply = jnp.dot(recv_onehot, w, preferred_element_type=f32).astype(jnp.bfloat16)
    reply, halos = lax.optimization_barrier((reply, halos))
    back = lax.all_to_all(reply.reshape(devices, capacity, 64), ("gx", "gy"), 0, 0, tiled=True)
    back = back.reshape(devices * capacity, 64)
    values = jnp.dot(place, back, preferred_element_type=f32).astype(jnp.bfloat16)
    return jnp.dot(values, back_lift, preferred_element_type=f32), halos


def body(field, inv_material, stiffness, lift, projection, back_lift, op_blocks, op_columns, panel_dest, panel_anchor):
    f32, bf16 = jnp.float32, jnp.bfloat16
    ex_n, ey_n, ez_n = field.shape[:3]
    n = ex_n * ey_n * ez_n
    devices = lax.axis_size("gx") * lax.axis_size("gy")
    panels = ex_n * ey_n
    capacity = max(2, 2 * panels // devices)
    dest = panel_dest[:, 0]
    hit = (dest[:, None] == jnp.arange(devices, dtype=jnp.int32)[None, :]).astype(jnp.int32)
    ranks = jnp.cumsum(hit, axis=0)
    slots = jnp.sum(hit * (ranks - 1), axis=1)
    position = dest * capacity + slots
    place = (position[:, None] == jnp.arange(devices * capacity, dtype=jnp.int32)[None, :]).astype(bf16)
    code = jnp.einsum("pr,p->r", place, (panel_anchor + 1).astype(bf16), preferred_element_type=f32).astype(bf16)
    recv_code = lax.all_to_all(code.reshape(devices, capacity), ("gx", "gy"), 0, 0, tiled=True)
    recv_code = recv_code.reshape(devices * capacity)
    levels = (jnp.arange(NBLK, dtype=jnp.int32) + 1).astype(bf16)
    recv_onehot = (recv_code[:, None] == levels[None, :]).astype(bf16)

    sel = trace_selector()
    lift_pad = pad_faces(lift)
    proj_pad = jnp.concatenate([projection, jnp.zeros((LANE - 96, 64), bf16)], 0)
    inv = inv_material.reshape(n, 1)
    zero_z = jnp.zeros((ex_n, ey_n, 1, LANE), bf16)

    def evaluate(section):
        sb = section.reshape(n, 384).astype(bf16)
        t = jnp.dot(sb, sel, preferred_element_type=f32).astype(bf16)
        t4 = t.reshape(ex_n, ey_n, ez_n, 6 * LANE)
        xlo, xhi = t4[..., 0:LANE], t4[..., LANE:2 * LANE]
        ylo, yhi = t4[..., 2 * LANE:3 * LANE], t4[..., 3 * LANE:4 * LANE]
        zlo, zhi = t4[..., 4 * LANE:5 * LANE], t4[..., 5 * LANE:6 * LANE]
        halo_xl = shift_in(xhi[ex_n - 1:], "gx", 0, True)
        halo_xr = shift_in(xlo[:1], "gx", 0, False)
        halo_yl = shift_in(yhi[:, ey_n - 1:], "gy", 1, True)
        halo_yr = shift_in(ylo[:, :1], "gy", 1, False)
        tops = zhi[:, :, ez_n - 1, :].reshape(panels, LANE)
        bvals, (halo_xl, halo_xr, halo_yl, halo_yr) = boundary_term(
            tops, proj_pad, back_lift, op_blocks, op_columns, place, recv_onehot, devices, capacity,
            (halo_xl, halo_xr, halo_yl, halo_yr))
        total = rate_call(
            sb, t,
            halo_xl.reshape(ey_n * ez_n, LANE), halo_xr.reshape(ey_n * ez_n, LANE),
            halo_yl.reshape(ex_n * ez_n, LANE), halo_yr.reshape(ex_n * ez_n, LANE),
            stiffness, lift_pad, (ex_n, ey_n, ez_n),
        ).reshape(ex_n, ey_n, ez_n, 384)
        top = total[:, :, ez_n - 1:, :] + bvals.reshape(ex_n, ey_n, 1, 384)
        total = jnp.concatenate([total[:, :, :ez_n - 1, :], top], 2)
        return inv_material[..., None] * total

    k_one = evaluate(field)
    k_two = evaluate(field + step_size / 2 * k_one)
    k_three = evaluate(field + step_size / 2 * k_two)
    k_four = evaluate(field + step_size * k_three)
    return field + step_size / 6 * (k_one + 2.0 * k_two + 2.0 * k_three + k_four)


def solution(mesh):
    return jax.shard_map(
        body,
        mesh=mesh,
        in_specs=(
            P("gx", "gy", None, None),
            P("gx", "gy", None),
            P(), P(), P(), P(), P(), P(),
            P(("gx", "gy"), None),
            P(("gx", "gy")),
        ),
        out_specs=P("gx", "gy", None, None),
        check_vma=False,
    )
```

```python
import jax
import jax.numpy as jnp
from jax import lax
from jax.sharding import PartitionSpec as P
from jax.experimental import pallas as pl
from jax.experimental.pallas import tpu as pltpu
import functools

NBLK = 8
LANE = 128

step_size = 0.25


def rate_kernel(ex_n, ey_n, ez_n, sb_ref, t_ref, xl_ref, xr_ref, yl_ref, yr_ref, stiff_ref, lift_ref, out_ref):
    f32, bf16 = jnp.float32, jnp.bfloat16
    n = ex_n * ey_n * ez_n
    plane = ey_n * ez_n
    row = lax.broadcasted_iota(jnp.int32, (n, LANE), 0)
    ez = row % ez_n
    parts = []
    own = t_ref[:, 0:LANE].astype(f32)
    nb = jnp.concatenate([xl_ref[...], t_ref[0:n - plane, LANE:2 * LANE]], 0).astype(f32)
    parts.append((nb - own).astype(bf16))
    own = t_ref[:, LANE:2 * LANE].astype(f32)
    nb = jnp.concatenate([t_ref[plane:n, 0:LANE], xr_ref[...]], 0).astype(f32)
    parts.append((nb - own).astype(bf16))
    own = t_ref[:, 2 * LANE:3 * LANE].astype(f32)
    pieces = []
    for ex in range(ex_n):
        pieces.append(yl_ref[ex * ez_n:(ex + 1) * ez_n, :])
        pieces.append(t_ref[ex * plane:(ex + 1) * plane - ez_n, 3 * LANE:4 * LANE])
    nb = jnp.concatenate(pieces, 0).astype(f32)
    parts.append((nb - own).astype(bf16))
    own = t_ref[:, 3 * LANE:4 * LANE].astype(f32)
    pieces = []
    for ex in range(ex_n):
        pieces.append(t_ref[ex * plane + ez_n:(ex + 1) * plane, 2 * LANE:3 * LANE])
        pieces.append(yr_ref[ex * ez_n:(ex + 1) * ez_n, :])
    nb = jnp.concatenate(pieces, 0).astype(f32)
    parts.append((nb - own).astype(bf16))
    zlo = t_ref[:, 4 * LANE:5 * LANE].astype(f32)
    zhi = t_ref[:, 5 * LANE:6 * LANE].astype(f32)
    nb = jnp.where(ez == 0, 0.0, pltpu.roll(zhi, 1, 0))
    parts.append((nb - zlo).astype(bf16))
    nb = jnp.where(ez == ez_n - 1, 0.0, pltpu.roll(zlo, n - 1, 0))
    parts.append((nb - zhi).astype(bf16))
    jumps = jnp.concatenate(parts, -1)
    out_ref[...] = (jnp.dot(sb_ref[...], stiff_ref[...], preferred_element_type=f32)
                    + jnp.dot(jumps, lift_ref[...], preferred_element_type=f32))


def rate_call(sb, t, xl, xr, yl, yr, stiff, lift_pad, dims):
    ex_n, ey_n, ez_n = dims
    n = ex_n * ey_n * ez_n
    vm = pl.BlockSpec(memory_space=pltpu.VMEM)
    flops = 2 * n * 384 * (384 + 6 * LANE)
    return pl.pallas_call(
        functools.partial(rate_kernel, ex_n, ey_n, ez_n),
        out_shape=jax.ShapeDtypeStruct((n, 384), jnp.float32),
        in_specs=[vm] * 8,
        out_specs=vm,
        cost_estimate=pl.CostEstimate(flops=flops, bytes_accessed=n * (384 * 2 + 768 * 2 + 384 * 4), transcendentals=0),
    )(sb, t, xl, xr, yl, yr, stiff, lift_pad)


def shift_in(arr, axis, dim, lower):
    count = lax.axis_size(axis)
    if lower:
        pairs = [(i, i + 1) for i in range(count - 1)]
    else:
        pairs = [(i + 1, i) for i in range(count - 1)]
    return lax.ppermute(arr, axis, pairs)


def trace_selector():
    rows = lax.broadcasted_iota(jnp.int32, (384, 6 * LANE), 0)
    cols = lax.broadcasted_iota(jnp.int32, (384, 6 * LANE), 1)
    face, j = cols // LANE, cols % LANE
    comp, p, q = j // 16, (j // 4) % 4, j % 4
    side = jnp.where(face % 2 == 0, 0, 3)
    ax = face // 2
    a = jnp.where(ax == 0, side, p)
    b = jnp.where(ax == 0, p, jnp.where(ax == 1, side, q))
    c = jnp.where(ax == 2, side, q)
    src = comp * 64 + a * 16 + b * 4 + c
    return ((rows == src) & (j < 96)).astype(jnp.bfloat16)


def pad_faces(mat):
    k = mat.shape[1]
    zero = jnp.zeros((LANE - 96, k), mat.dtype)
    parts = []
    for f in range(6):
        parts += [mat[96 * f:96 * (f + 1)], zero]
    return jnp.concatenate(parts, 0)

def post_kernel(ez_n, coef_next, mult, final, *refs):
    f32, bf16 = jnp.float32, jnp.bfloat16
    if final:
        total_ref, bvals_ref, inv_ref, field_ref, acc_ref, out_ref = refs
    elif mult is None:
        total_ref, bvals_ref, inv_ref, field_ref, sel_ref, acc_out, sb_out, t_out = refs
    else:
        total_ref, bvals_ref, inv_ref, field_ref, acc_ref, sel_ref, acc_out, sb_out, t_out = refs
    n, width = total_ref.shape
    tot = total_ref[...].reshape(n // ez_n, ez_n, width)
    top = lax.broadcasted_iota(jnp.int32, tot.shape, 1) == ez_n - 1
    tot = jnp.where(top, tot + bvals_ref[...][:, None, :], tot).reshape(n, width)
    k = inv_ref[...] * tot
    if mult is None:
        acc = k
    else:
        acc = acc_ref[...] + mult * k if mult != 1.0 else acc_ref[...] + k
    if final:
        out_ref[...] = field_ref[...] + step_size / 6 * acc
        return
    acc_out[...] = acc
    sb = (field_ref[...] + coef_next * k).astype(bf16)
    sb_out[...] = sb
    t_out[...] = jnp.dot(sb, sel_ref[...], preferred_element_type=f32).astype(bf16)


def post_call(total, bvals, inv, field, acc, sel, ez_n, coef_next, mult, final):
    n, width = total.shape
    vm = pl.BlockSpec(memory_space=pltpu.VMEM)
    ins = [total, bvals, inv, field] + ([acc] if acc is not None else []) + ([] if final else [sel])
    if final:
        outs = jax.ShapeDtypeStruct((n, width), jnp.float32)
        out_specs = vm
    else:
        outs = (jax.ShapeDtypeStruct((n, width), jnp.float32), jax.ShapeDtypeStruct((n, width), jnp.bfloat16),
                jax.ShapeDtypeStruct((n, 6 * LANE), jnp.bfloat16))
        out_specs = (vm, vm, vm)
    return pl.pallas_call(
        functools.partial(post_kernel, ez_n, coef_next, mult, final),
        out_shape=outs,
        in_specs=[vm] * len(ins),
        out_specs=out_specs,
        cost_estimate=pl.CostEstimate(flops=2 * n * width * 6 * LANE, bytes_accessed=n * width * 4 * 6, transcendentals=0),
    )(*ins)


def boundary_term(tops, proj_pad, back_lift, op_blocks, op_columns, place, recv_onehot, devices, capacity, halos):
    f32 = jnp.float32
    u = jnp.dot(tops, proj_pad, preferred_element_type=f32).astype(jnp.bfloat16)
    send_u = jnp.einsum("pr,pc->rc", place, u, preferred_element_type=f32).astype(jnp.bfloat16)
    recv_u = lax.all_to_all(send_u.reshape(devices, capacity, 64), ("gx", "gy"), 0, 0, tiled=True)
    recv_u = recv_u.reshape(devices * capacity, 64)
    grid = jnp.einsum("rb,rc->bc", recv_onehot, recv_u, preferred_element_type=f32).astype(jnp.bfloat16)
    select = (op_columns[:, :, None] == jnp.arange(NBLK, dtype=jnp.int32)[None, None, :]).astype(jnp.bfloat16)
    gsel = jnp.einsum("ikj,jc->ikc", select, grid, preferred_element_type=f32).astype(jnp.bfloat16)
    w = jnp.einsum("ikc,ikce->ie", gsel, op_blocks, preferred_element_type=f32).astype(jnp.bfloat16)
    reply = jnp.dot(recv_onehot, w, preferred_element_type=f32).astype(jnp.bfloat16)
    reply, halos = lax.optimization_barrier((reply, halos))
    back = lax.all_to_all(reply.reshape(devices, capacity, 64), ("gx", "gy"), 0, 0, tiled=True)
    back = back.reshape(devices * capacity, 64)
    values = jnp.dot(place, back, preferred_element_type=f32).astype(jnp.bfloat16)
    return jnp.dot(values, back_lift, preferred_element_type=f32), halos


def body(field, inv_material, stiffness, lift, projection, back_lift, op_blocks, op_columns, panel_dest, panel_anchor):
    f32, bf16 = jnp.float32, jnp.bfloat16
    ex_n, ey_n, ez_n = field.shape[:3]
    n = ex_n * ey_n * ez_n
    devices = lax.axis_size("gx") * lax.axis_size("gy")
    panels = ex_n * ey_n
    capacity = max(2, 2 * panels // devices)
    dest = panel_dest[:, 0]
    hit = (dest[:, None] == jnp.arange(devices, dtype=jnp.int32)[None, :]).astype(jnp.int32)
    ranks = jnp.cumsum(hit, axis=0)
    slots = jnp.sum(hit * (ranks - 1), axis=1)
    position = dest * capacity + slots
    place = (position[:, None] == jnp.arange(devices * capacity, dtype=jnp.int32)[None, :]).astype(bf16)
    code = jnp.einsum("pr,p->r", place, (panel_anchor + 1).astype(bf16), preferred_element_type=f32).astype(bf16)
    recv_code = lax.all_to_all(code.reshape(devices, capacity), ("gx", "gy"), 0, 0, tiled=True)
    recv_code = recv_code.reshape(devices * capacity)
    levels = (jnp.arange(NBLK, dtype=jnp.int32) + 1).astype(bf16)
    recv_onehot = (recv_code[:, None] == levels[None, :]).astype(bf16)

    sel = trace_selector()
    lift_pad = pad_faces(lift)
    proj_pad = jnp.concatenate([projection, jnp.zeros((LANE - 96, 64), bf16)], 0)
    inv = inv_material.reshape(n, 1)
    zero_z = jnp.zeros((ex_n, ey_n, 1, LANE), bf16)

    fieldf = field.reshape(n, 384)
    inv = inv_material.reshape(n, 1)

    def stage(sb, t):
        t4 = t.reshape(ex_n, ey_n, ez_n, 6 * LANE)
        xlo, xhi = t4[..., 0:LANE], t4[..., LANE:2 * LANE]
        ylo, yhi = t4[..., 2 * LANE:3 * LANE], t4[..., 3 * LANE:4 * LANE]
        zhi = t4[..., 5 * LANE:6 * LANE]
        halo_xl = shift_in(xhi[ex_n - 1:], "gx", 0, True)
        halo_xr = shift_in(xlo[:1], "gx", 0, False)
        halo_yl = shift_in(yhi[:, ey_n - 1:], "gy", 1, True)
        halo_yr = shift_in(ylo[:, :1], "gy", 1, False)
        tops = zhi[:, :, ez_n - 1, :].reshape(panels, LANE)
        bvals, (halo_xl, halo_xr, halo_yl, halo_yr) = boundary_term(
            tops, proj_pad, back_lift, op_blocks, op_columns, place, recv_onehot, devices, capacity,
            (halo_xl, halo_xr, halo_yl, halo_yr))
        total = rate_call(
            sb, t,
            halo_xl.reshape(ey_n * ez_n, LANE), halo_xr.reshape(ey_n * ez_n, LANE),
            halo_yl.reshape(ex_n * ez_n, LANE), halo_yr.reshape(ex_n * ez_n, LANE),
            stiffness, lift_pad, (ex_n, ey_n, ez_n),
        )
        return total, bvals

    sb = fieldf.astype(bf16)
    t = jnp.dot(sb, sel, preferred_element_type=f32).astype(bf16)
    total, bvals = stage(sb, t)
    acc, sb, t = post_call(total, bvals, inv, fieldf, None, sel, ez_n, step_size / 2, None, False)
    total, bvals = stage(sb, t)
    acc, sb, t = post_call(total, bvals, inv, fieldf, acc, sel, ez_n, step_size / 2, 2.0, False)
    total, bvals = stage(sb, t)
    acc, sb, t = post_call(total, bvals, inv, fieldf, acc, sel, ez_n, step_size, 2.0, False)
    total, bvals = stage(sb, t)
    out = post_call(total, bvals, inv, fieldf, acc, None, ez_n, None, 1.0, True)
    return out.reshape(field.shape)


def solution(mesh):
    return jax.shard_map(
        body,
        mesh=mesh,
        in_specs=(
            P("gx", "gy", None, None),
            P("gx", "gy", None),
            P(), P(), P(), P(), P(), P(),
            P(("gx", "gy"), None),
            P(("gx", "gy")),
        ),
        out_specs=P("gx", "gy", None, None),
        check_vma=False,
    )
```

```python
import jax
import jax.numpy as jnp
from jax import lax
from jax.sharding import PartitionSpec as P
from jax.experimental import pallas as pl
from jax.experimental.pallas import tpu as pltpu
import functools

NBLK = 8
LANE = 128

step_size = 0.25


def rate_kernel(ex_n, ey_n, ez_n, sb_ref, t_ref, xl_ref, xr_ref, yl_ref, yr_ref, stiff_ref, lift_ref, out_ref):
    f32, bf16 = jnp.float32, jnp.bfloat16
    n = ex_n * ey_n * ez_n
    plane = ey_n * ez_n
    row = lax.broadcasted_iota(jnp.int32, (n, LANE), 0)
    ez = row % ez_n
    parts = []
    own = t_ref[:, 0:LANE].astype(f32)
    nb = jnp.concatenate([xl_ref[...], t_ref[0:n - plane, LANE:2 * LANE]], 0).astype(f32)
    parts.append((nb - own).astype(bf16))
    own = t_ref[:, LANE:2 * LANE].astype(f32)
    nb = jnp.concatenate([t_ref[plane:n, 0:LANE], xr_ref[...]], 0).astype(f32)
    parts.append((nb - own).astype(bf16))
    own = t_ref[:, 2 * LANE:3 * LANE].astype(f32)
    pieces = []
    for ex in range(ex_n):
        pieces.append(yl_ref[ex * ez_n:(ex + 1) * ez_n, :])
        pieces.append(t_ref[ex * plane:(ex + 1) * plane - ez_n, 3 * LANE:4 * LANE])
    nb = jnp.concatenate(pieces, 0).astype(f32)
    parts.append((nb - own).astype(bf16))
    own = t_ref[:, 3 * LANE:4 * LANE].astype(f32)
    pieces = []
    for ex in range(ex_n):
        pieces.append(t_ref[ex * plane + ez_n:(ex + 1) * plane, 2 * LANE:3 * LANE])
        pieces.append(yr_ref[ex * ez_n:(ex + 1) * ez_n, :])
    nb = jnp.concatenate(pieces, 0).astype(f32)
    parts.append((nb - own).astype(bf16))
    zlo = t_ref[:, 4 * LANE:5 * LANE].astype(f32)
    zhi = t_ref[:, 5 * LANE:6 * LANE].astype(f32)
    nb = jnp.where(ez == 0, 0.0, pltpu.roll(zhi, 1, 0))
    parts.append((nb - zlo).astype(bf16))
    nb = jnp.where(ez == ez_n - 1, 0.0, pltpu.roll(zlo, n - 1, 0))
    parts.append((nb - zhi).astype(bf16))
    jumps = jnp.concatenate(parts, -1)
    out_ref[...] = (jnp.dot(sb_ref[...], stiff_ref[...], preferred_element_type=f32)
                    + jnp.dot(jumps, lift_ref[...], preferred_element_type=f32))


def rate_call(sb, t, xl, xr, yl, yr, stiff, lift_pad, dims):
    ex_n, ey_n, ez_n = dims
    n = ex_n * ey_n * ez_n
    vm = pl.BlockSpec(memory_space=pltpu.VMEM)
    flops = 2 * n * 384 * (384 + 6 * LANE)
    return pl.pallas_call(
        functools.partial(rate_kernel, ex_n, ey_n, ez_n),
        out_shape=jax.ShapeDtypeStruct((n, 384), jnp.float32),
        in_specs=[vm] * 8,
        out_specs=vm,
        cost_estimate=pl.CostEstimate(flops=flops, bytes_accessed=n * (384 * 2 + 768 * 2 + 384 * 4), transcendentals=0),
    )(sb, t, xl, xr, yl, yr, stiff, lift_pad)


def shift_in(arr, axis, dim, lower):
    count = lax.axis_size(axis)
    if lower:
        pairs = [(i, i + 1) for i in range(count - 1)]
    else:
        pairs = [(i + 1, i) for i in range(count - 1)]
    return lax.ppermute(arr, axis, pairs)


def trace_selector():
    rows = lax.broadcasted_iota(jnp.int32, (384, 6 * LANE), 0)
    cols = lax.broadcasted_iota(jnp.int32, (384, 6 * LANE), 1)
    face, j = cols // LANE, cols % LANE
    comp, p, q = j // 16, (j // 4) % 4, j % 4
    side = jnp.where(face % 2 == 0, 0, 3)
    ax = face // 2
    a = jnp.where(ax == 0, side, p)
    b = jnp.where(ax == 0, p, jnp.where(ax == 1, side, q))
    c = jnp.where(ax == 2, side, q)
    src = comp * 64 + a * 16 + b * 4 + c
    return ((rows == src) & (j < 96)).astype(jnp.bfloat16)


def pad_faces(mat):
    k = mat.shape[1]
    zero = jnp.zeros((LANE - 96, k), mat.dtype)
    parts = []
    for f in range(6):
        parts += [mat[96 * f:96 * (f + 1)], zero]
    return jnp.concatenate(parts, 0)

def step_kernel(dims, coef_next, mult, final, *refs):
    f32, bf16 = jnp.float32, jnp.bfloat16
    ex_n, ey_n, ez_n = dims
    refs = list(refs)
    sb_ref, t_ref, xl_ref, xr_ref, yl_ref, yr_ref, stiff_ref, lift_ref, bvals_ref, inv_ref, field_ref = refs[:11]
    refs = refs[11:]
    acc_ref = refs.pop(0) if mult is not None else None
    if final:
        (out_ref,) = refs
    else:
        sel_ref, seltop_ref, proj_ref, placet_ref, acc_out, sb_out, t_out, send_out = refs
    n = ex_n * ey_n * ez_n
    plane = ey_n * ez_n
    row = lax.broadcasted_iota(jnp.int32, (n, LANE), 0)
    ez = row % ez_n
    parts = []
    own = t_ref[:, 0:LANE].astype(f32)
    nb = jnp.concatenate([xl_ref[...], t_ref[0:n - plane, LANE:2 * LANE]], 0).astype(f32)
    parts.append((nb - own).astype(bf16))
    own = t_ref[:, LANE:2 * LANE].astype(f32)
    nb = jnp.concatenate([t_ref[plane:n, 0:LANE], xr_ref[...]], 0).astype(f32)
    parts.append((nb - own).astype(bf16))
    own = t_ref[:, 2 * LANE:3 * LANE].astype(f32)
    pieces = []
    for ex in range(ex_n):
        pieces.append(yl_ref[ex * ez_n:(ex + 1) * ez_n, :])
        pieces.append(t_ref[ex * plane:(ex + 1) * plane - ez_n, 3 * LANE:4 * LANE])
    nb = jnp.concatenate(pieces, 0).astype(f32)
    parts.append((nb - own).astype(bf16))
    own = t_ref[:, 3 * LANE:4 * LANE].astype(f32)
    pieces = []
    for ex in range(ex_n):
        pieces.append(t_ref[ex * plane + ez_n:(ex + 1) * plane, 2 * LANE:3 * LANE])
        pieces.append(yr_ref[ex * ez_n:(ex + 1) * ez_n, :])
    nb = jnp.concatenate(pieces, 0).astype(f32)
    parts.append((nb - own).astype(bf16))
    zlo = t_ref[:, 4 * LANE:5 * LANE].astype(f32)
    zhi = t_ref[:, 5 * LANE:6 * LANE].astype(f32)
    nb = jnp.where(ez == 0, 0.0, pltpu.roll(zhi, 1, 0))
    parts.append((nb - zlo).astype(bf16))
    nb = jnp.where(ez == ez_n - 1, 0.0, pltpu.roll(zlo, n - 1, 0))
    parts.append((nb - zhi).astype(bf16))
    jumps = jnp.concatenate(parts, -1)
    tot = (jnp.dot(sb_ref[...], stiff_ref[...], preferred_element_type=f32)
           + jnp.dot(jumps, lift_ref[...], preferred_element_type=f32))
    width = tot.shape[1]
    tot = tot.reshape(n // ez_n, ez_n, width)
    top = lax.broadcasted_iota(jnp.int32, tot.shape, 1) == ez_n - 1
    tot = jnp.where(top, tot + bvals_ref[...][:, None, :], tot).reshape(n, width)
    k = inv_ref[...] * tot
    if mult is None:
        acc = k
    elif mult == 1.0:
        acc = acc_ref[...] + k
    else:
        acc = acc_ref[...] + mult * k
    if final:
        out_ref[...] = field_ref[...] + step_size / 6 * acc
        return
    acc_out[...] = acc
    sb = (field_ref[...] + coef_next * k).astype(bf16)
    sb_out[...] = sb
    t = jnp.dot(sb, sel_ref[...], preferred_element_type=f32).astype(bf16)
    t_out[...] = t
    tops = jnp.dot(seltop_ref[...], t[:, 5 * LANE:6 * LANE], preferred_element_type=f32).astype(bf16)
    u = jnp.dot(tops, proj_ref[...], preferred_element_type=f32).astype(bf16)
    send_out[...] = jnp.dot(placet_ref[...], u, preferred_element_type=f32).astype(bf16)


def step_call(ins, dims, coef_next, mult, final, slots):
    n = dims[0] * dims[1] * dims[2]
    vm = pl.BlockSpec(memory_space=pltpu.VMEM)
    if final:
        outs = jax.ShapeDtypeStruct((n, 384), jnp.float32)
        out_specs = vm
    else:
        outs = (jax.ShapeDtypeStruct((n, 384), jnp.float32), jax.ShapeDtypeStruct((n, 384), jnp.bfloat16),
                jax.ShapeDtypeStruct((n, 6 * LANE), jnp.bfloat16), jax.ShapeDtypeStruct((slots, 64), jnp.bfloat16))
        out_specs = (vm, vm, vm, vm)
    flops = 2 * n * 384 * (384 + 12 * LANE)
    return pl.pallas_call(
        functools.partial(step_kernel, dims, coef_next, mult, final),
        out_shape=outs,
        in_specs=[vm] * len(ins),
        out_specs=out_specs,
        cost_estimate=pl.CostEstimate(flops=flops, bytes_accessed=n * 384 * 4 * 6, transcendentals=0),
    )(*ins)


def exchange(send_u, back_lift, op_blocks, op_columns, place, recv_onehot, devices, capacity, halos):
    f32 = jnp.float32
    recv_u = lax.all_to_all(send_u.reshape(devices, capacity, 64), ("gx", "gy"), 0, 0, tiled=True)
    recv_u = recv_u.reshape(devices * capacity, 64)
    grid = jnp.einsum("rb,rc->bc", recv_onehot, recv_u, preferred_element_type=f32).astype(jnp.bfloat16)
    select = (op_columns[:, :, None] == jnp.arange(NBLK, dtype=jnp.int32)[None, None, :]).astype(jnp.bfloat16)
    gsel = jnp.einsum("ikj,jc->ikc", select, grid, preferred_element_type=f32).astype(jnp.bfloat16)
    w = jnp.einsum("ikc,ikce->ie", gsel, op_blocks, preferred_element_type=f32).astype(jnp.bfloat16)
    reply = jnp.dot(recv_onehot, w, preferred_element_type=f32).astype(jnp.bfloat16)
    reply, halos = lax.optimization_barrier((reply, halos))
    back = lax.all_to_all(reply.reshape(devices, capacity, 64), ("gx", "gy"), 0, 0, tiled=True)
    back = back.reshape(devices * capacity, 64)
    values = jnp.dot(place, back, preferred_element_type=f32).astype(jnp.bfloat16)
    return jnp.dot(values, back_lift, preferred_element_type=f32), halos


def body(field, inv_material, stiffness, lift, projection, back_lift, op_blocks, op_columns, panel_dest, panel_anchor):
    f32, bf16 = jnp.float32, jnp.bfloat16
    ex_n, ey_n, ez_n = field.shape[:3]
    n = ex_n * ey_n * ez_n
    devices = lax.axis_size("gx") * lax.axis_size("gy")
    panels = ex_n * ey_n
    capacity = max(2, 2 * panels // devices)
    dest = panel_dest[:, 0]
    hit = (dest[:, None] == jnp.arange(devices, dtype=jnp.int32)[None, :]).astype(jnp.int32)
    ranks = jnp.cumsum(hit, axis=0)
    slots = jnp.sum(hit * (ranks - 1), axis=1)
    position = dest * capacity + slots
    place = (position[:, None] == jnp.arange(devices * capacity, dtype=jnp.int32)[None, :]).astype(bf16)
    code = jnp.einsum("pr,p->r", place, (panel_anchor + 1).astype(bf16), preferred_element_type=f32).astype(bf16)
    recv_code = lax.all_to_all(code.reshape(devices, capacity), ("gx", "gy"), 0, 0, tiled=True)
    recv_code = recv_code.reshape(devices * capacity)
    levels = (jnp.arange(NBLK, dtype=jnp.int32) + 1).astype(bf16)
    recv_onehot = (recv_code[:, None] == levels[None, :]).astype(bf16)

    sel = trace_selector()
    lift_pad = pad_faces(lift)
    proj_pad = jnp.concatenate([projection, jnp.zeros((LANE - 96, 64), bf16)], 0)
    inv = inv_material.reshape(n, 1)
    zero_z = jnp.zeros((ex_n, ey_n, 1, LANE), bf16)

    fieldf = field.reshape(n, 384)
    inv = inv_material.reshape(n, 1)
    placet = place.T
    rows = lax.broadcasted_iota(jnp.int32, (panels, n), 1)
    seltop = (rows == lax.broadcasted_iota(jnp.int32, (panels, n), 0) * ez_n + ez_n - 1).astype(bf16)
    dims = (ex_n, ey_n, ez_n)

    sb = fieldf.astype(bf16)
    t = jnp.dot(sb, sel, preferred_element_type=f32).astype(bf16)
    tops = t.reshape(ex_n, ey_n, ez_n, 6 * LANE)[:, :, ez_n - 1, 5 * LANE:6 * LANE].reshape(panels, LANE)
    u = jnp.dot(tops, proj_pad, preferred_element_type=f32).astype(bf16)
    send = jnp.dot(placet, u, preferred_element_type=f32).astype(bf16)
    acc = None
    coefs = (step_size / 2, step_size / 2, step_size, None)
    mults = (None, 2.0, 2.0, 1.0)
    for i in range(4):
        t4 = t.reshape(ex_n, ey_n, ez_n, 6 * LANE)
        xlo, xhi = t4[..., 0:LANE], t4[..., LANE:2 * LANE]
        ylo, yhi = t4[..., 2 * LANE:3 * LANE], t4[..., 3 * LANE:4 * LANE]
        halos = (
            shift_in(xhi[ex_n - 1:], "gx", 0, True).reshape(ey_n * ez_n, LANE),
            shift_in(xlo[:1], "gx", 0, False).reshape(ey_n * ez_n, LANE),
            shift_in(yhi[:, ey_n - 1:], "gy", 1, True).reshape(ex_n * ez_n, LANE),
            shift_in(ylo[:, :1], "gy", 1, False).reshape(ex_n * ez_n, LANE),
        )
        bvals, halos = exchange(send, back_lift, op_blocks, op_columns, place, recv_onehot, devices, capacity, halos)
        final = i == 3
        ins = [sb, t, *halos, stiffness, lift_pad, bvals, inv, fieldf]
        if mults[i] is not None:
            ins.append(acc)
        if final:
            out = step_call(ins, dims, coefs[i], mults[i], True, devices * capacity)
        else:
            ins += [sel, seltop, proj_pad, placet]
            acc, sb, t, send = step_call(ins, dims, coefs[i], mults[i], False, devices * capacity)
    return out.reshape(field.shape)


def solution(mesh):
    return jax.shard_map(
        body,
        mesh=mesh,
        in_specs=(
            P("gx", "gy", None, None),
            P("gx", "gy", None),
            P(), P(), P(), P(), P(), P(),
            P(("gx", "gy"), None),
            P(("gx", "gy")),
        ),
        out_specs=P("gx", "gy", None, None),
        check_vma=False,
    )
```

```python
import jax
import jax.numpy as jnp
from jax import lax
from jax.sharding import PartitionSpec as P
from jax.experimental import pallas as pl
from jax.experimental.pallas import tpu as pltpu
import functools

NBLK = 8
LANE = 128

step_size = 0.25


def rate_kernel(ex_n, ey_n, ez_n, sb_ref, t_ref, xl_ref, xr_ref, yl_ref, yr_ref, stiff_ref, lift_ref, out_ref):
    f32, bf16 = jnp.float32, jnp.bfloat16
    n = ex_n * ey_n * ez_n
    plane = ey_n * ez_n
    row = lax.broadcasted_iota(jnp.int32, (n, LANE), 0)
    ez = row % ez_n
    parts = []
    own = t_ref[:, 0:LANE].astype(f32)
    nb = jnp.concatenate([xl_ref[...], t_ref[0:n - plane, LANE:2 * LANE]], 0).astype(f32)
    parts.append((nb - own).astype(bf16))
    own = t_ref[:, LANE:2 * LANE].astype(f32)
    nb = jnp.concatenate([t_ref[plane:n, 0:LANE], xr_ref[...]], 0).astype(f32)
    parts.append((nb - own).astype(bf16))
    own = t_ref[:, 2 * LANE:3 * LANE].astype(f32)
    pieces = []
    for ex in range(ex_n):
        pieces.append(yl_ref[ex * ez_n:(ex + 1) * ez_n, :])
        pieces.append(t_ref[ex * plane:(ex + 1) * plane - ez_n, 3 * LANE:4 * LANE])
    nb = jnp.concatenate(pieces, 0).astype(f32)
    parts.append((nb - own).astype(bf16))
    own = t_ref[:, 3 * LANE:4 * LANE].astype(f32)
    pieces = []
    for ex in range(ex_n):
        pieces.append(t_ref[ex * plane + ez_n:(ex + 1) * plane, 2 * LANE:3 * LANE])
        pieces.append(yr_ref[ex * ez_n:(ex + 1) * ez_n, :])
    nb = jnp.concatenate(pieces, 0).astype(f32)
    parts.append((nb - own).astype(bf16))
    zlo = t_ref[:, 4 * LANE:5 * LANE].astype(f32)
    zhi = t_ref[:, 5 * LANE:6 * LANE].astype(f32)
    nb = jnp.where(ez == 0, 0.0, pltpu.roll(zhi, 1, 0))
    parts.append((nb - zlo).astype(bf16))
    nb = jnp.where(ez == ez_n - 1, 0.0, pltpu.roll(zlo, n - 1, 0))
    parts.append((nb - zhi).astype(bf16))
    jumps = jnp.concatenate(parts, -1)
    out_ref[...] = (jnp.dot(sb_ref[...], stiff_ref[...], preferred_element_type=f32)
                    + jnp.dot(jumps, lift_ref[...], preferred_element_type=f32))


def rate_call(sb, t, xl, xr, yl, yr, stiff, lift_pad, dims):
    ex_n, ey_n, ez_n = dims
    n = ex_n * ey_n * ez_n
    vm = pl.BlockSpec(memory_space=pltpu.VMEM)
    flops = 2 * n * 384 * (384 + 6 * LANE)
    return pl.pallas_call(
        functools.partial(rate_kernel, ex_n, ey_n, ez_n),
        out_shape=jax.ShapeDtypeStruct((n, 384), jnp.float32),
        in_specs=[vm] * 8,
        out_specs=vm,
        cost_estimate=pl.CostEstimate(flops=flops, bytes_accessed=n * (384 * 2 + 768 * 2 + 384 * 4), transcendentals=0),
    )(sb, t, xl, xr, yl, yr, stiff, lift_pad)


def shift_in(arr, axis, dim, lower):
    count = lax.axis_size(axis)
    if lower:
        pairs = [(i, i + 1) for i in range(count - 1)]
    else:
        pairs = [(i + 1, i) for i in range(count - 1)]
    return lax.ppermute(arr, axis, pairs)


def trace_selector():
    rows = lax.broadcasted_iota(jnp.int32, (384, 6 * LANE), 0)
    cols = lax.broadcasted_iota(jnp.int32, (384, 6 * LANE), 1)
    face, j = cols // LANE, cols % LANE
    comp, p, q = j // 16, (j // 4) % 4, j % 4
    side = jnp.where(face % 2 == 0, 0, 3)
    ax = face // 2
    a = jnp.where(ax == 0, side, p)
    b = jnp.where(ax == 0, p, jnp.where(ax == 1, side, q))
    c = jnp.where(ax == 2, side, q)
    src = comp * 64 + a * 16 + b * 4 + c
    return ((rows == src) & (j < 96)).astype(jnp.bfloat16)


def pad_faces(mat):
    k = mat.shape[1]
    zero = jnp.zeros((LANE - 96, k), mat.dtype)
    parts = []
    for f in range(6):
        parts += [mat[96 * f:96 * (f + 1)], zero]
    return jnp.concatenate(parts, 0)


def boundary_term(tops, proj_pad, back_lift, op_blocks, op_columns, place, recv_onehot, devices, capacity, halos):
    f32 = jnp.float32
    u = jnp.dot(tops, proj_pad, preferred_element_type=f32).astype(jnp.bfloat16)
    send_u = jnp.einsum("pr,pc->rc", place, u, preferred_element_type=f32).astype(jnp.bfloat16)
    recv_u = lax.all_to_all(send_u.reshape(devices, capacity, 64), ("gx", "gy"), 0, 0, tiled=True)
    recv_u = recv_u.reshape(devices * capacity, 64)
    grid = jnp.einsum("rb,rc->bc", recv_onehot, recv_u, preferred_element_type=f32).astype(jnp.bfloat16)
    xsend, yhalos = halos
    grid, xsend = lax.optimization_barrier((grid, xsend))
    xhalos = (shift_in(xsend[0], "gx", 0, True), shift_in(xsend[1], "gx", 0, False))
    select = (op_columns[:, :, None] == jnp.arange(NBLK, dtype=jnp.int32)[None, None, :]).astype(jnp.bfloat16)
    gsel = jnp.einsum("ikj,jc->ikc", select, grid, preferred_element_type=f32).astype(jnp.bfloat16)
    w = jnp.einsum("ikc,ikce->ie", gsel, op_blocks, preferred_element_type=f32).astype(jnp.bfloat16)
    reply = jnp.dot(recv_onehot, w, preferred_element_type=f32).astype(jnp.bfloat16)
    reply, yhalos = lax.optimization_barrier((reply, yhalos))
    halos = xhalos + yhalos
    back = lax.all_to_all(reply.reshape(devices, capacity, 64), ("gx", "gy"), 0, 0, tiled=True)
    back = back.reshape(devices * capacity, 64)
    values = jnp.dot(place, back, preferred_element_type=f32).astype(jnp.bfloat16)
    return jnp.dot(values, back_lift, preferred_element_type=f32), halos


def body(field, inv_material, stiffness, lift, projection, back_lift, op_blocks, op_columns, panel_dest, panel_anchor):
    f32, bf16 = jnp.float32, jnp.bfloat16
    ex_n, ey_n, ez_n = field.shape[:3]
    n = ex_n * ey_n * ez_n
    devices = lax.axis_size("gx") * lax.axis_size("gy")
    panels = ex_n * ey_n
    capacity = max(2, 2 * panels // devices)
    dest = panel_dest[:, 0]
    hit = (dest[:, None] == jnp.arange(devices, dtype=jnp.int32)[None, :]).astype(jnp.int32)
    ranks = jnp.cumsum(hit, axis=0)
    slots = jnp.sum(hit * (ranks - 1), axis=1)
    position = dest * capacity + slots
    place = (position[:, None] == jnp.arange(devices * capacity, dtype=jnp.int32)[None, :]).astype(bf16)
    code = jnp.einsum("pr,p->r", place, (panel_anchor + 1).astype(bf16), preferred_element_type=f32).astype(bf16)
    recv_code = lax.all_to_all(code.reshape(devices, capacity), ("gx", "gy"), 0, 0, tiled=True)
    recv_code = recv_code.reshape(devices * capacity)
    levels = (jnp.arange(NBLK, dtype=jnp.int32) + 1).astype(bf16)
    recv_onehot = (recv_code[:, None] == levels[None, :]).astype(bf16)

    sel = trace_selector()
    lift_pad = pad_faces(lift)
    proj_pad = jnp.concatenate([projection, jnp.zeros((LANE - 96, 64), bf16)], 0)
    inv = inv_material.reshape(n, 1)
    zero_z = jnp.zeros((ex_n, ey_n, 1, LANE), bf16)

    def evaluate(section):
        sb = section.reshape(n, 384).astype(bf16)
        t = jnp.dot(sb, sel, preferred_element_type=f32).astype(bf16)
        t4 = t.reshape(ex_n, ey_n, ez_n, 6 * LANE)
        xlo, xhi = t4[..., 0:LANE], t4[..., LANE:2 * LANE]
        ylo, yhi = t4[..., 2 * LANE:3 * LANE], t4[..., 3 * LANE:4 * LANE]
        zlo, zhi = t4[..., 4 * LANE:5 * LANE], t4[..., 5 * LANE:6 * LANE]
        halo_yl = shift_in(yhi[:, ey_n - 1:], "gy", 1, True)
        halo_yr = shift_in(ylo[:, :1], "gy", 1, False)
        tops = zhi[:, :, ez_n - 1, :].reshape(panels, LANE)
        bvals, (halo_xl, halo_xr, halo_yl, halo_yr) = boundary_term(
            tops, proj_pad, back_lift, op_blocks, op_columns, place, recv_onehot, devices, capacity,
            ((xhi[ex_n - 1:], xlo[:1]), (halo_yl, halo_yr)))
        total = rate_call(
            sb, t,
            halo_xl.reshape(ey_n * ez_n, LANE), halo_xr.reshape(ey_n * ez_n, LANE),
            halo_yl.reshape(ex_n * ez_n, LANE), halo_yr.reshape(ex_n * ez_n, LANE),
            stiffness, lift_pad, (ex_n, ey_n, ez_n),
        ).reshape(ex_n, ey_n, ez_n, 384)
        top = total[:, :, ez_n - 1:, :] + bvals.reshape(ex_n, ey_n, 1, 384)
        total = jnp.concatenate([total[:, :, :ez_n - 1, :], top], 2)
        return inv_material[..., None] * total

    k_one = evaluate(field)
    k_two = evaluate(field + step_size / 2 * k_one)
    k_three = evaluate(field + step_size / 2 * k_two)
    k_four = evaluate(field + step_size * k_three)
    return field + step_size / 6 * (k_one + 2.0 * k_two + 2.0 * k_three + k_four)


def solution(mesh):
    return jax.shard_map(
        body,
        mesh=mesh,
        in_specs=(
            P("gx", "gy", None, None),
            P("gx", "gy", None),
            P(), P(), P(), P(), P(), P(),
            P(("gx", "gy"), None),
            P(("gx", "gy")),
        ),
        out_specs=P("gx", "gy", None, None),
        check_vma=False,
    )
```

```python
import functools

import jax
import jax.numpy as jnp
from jax import lax
from jax.experimental import pallas as pl
from jax.experimental.pallas import tpu as pltpu
from jax.sharding import PartitionSpec as P

NBLK = 8
LANE = 128

step_size = 0.25


def shift_in(arr, axis, lower):
    count = lax.axis_size(axis)
    if lower:
        pairs = [(i, i + 1) for i in range(count - 1)]
    else:
        pairs = [(i + 1, i) for i in range(count - 1)]
    return lax.ppermute(arr, axis, pairs)


def trace_selector():
    rows = lax.broadcasted_iota(jnp.int32, (384, 6 * LANE), 0)
    cols = lax.broadcasted_iota(jnp.int32, (384, 6 * LANE), 1)
    face, j = cols // LANE, cols % LANE
    comp, p, q = j // 16, (j // 4) % 4, j % 4
    side = jnp.where(face % 2 == 0, 0, 3)
    ax = face // 2
    a = jnp.where(ax == 0, side, p)
    b = jnp.where(ax == 0, p, jnp.where(ax == 1, side, q))
    c = jnp.where(ax == 2, side, q)
    src = comp * 64 + a * 16 + b * 4 + c
    return ((rows == src) & (j < 96)).astype(jnp.bfloat16)


def pad_faces(mat):
    k = mat.shape[1]
    zero = jnp.zeros((LANE - 96, k), mat.dtype)
    parts = []
    for f in range(6):
        parts += [mat[96 * f:96 * (f + 1)], zero]
    return jnp.concatenate(parts, 0)


def vmem_call(kernel, ins, outs, flops, nbytes):
    vm = pl.BlockSpec(memory_space=pltpu.VMEM)
    multi = isinstance(outs, tuple)
    return pl.pallas_call(
        kernel,
        out_shape=outs,
        in_specs=[vm] * len(ins),
        out_specs=tuple(vm for _ in outs) if multi else vm,
        cost_estimate=pl.CostEstimate(flops=flops, bytes_accessed=nbytes, transcendentals=0),
    )(*ins)


def rate_kernel(dims, coef_next, mult, final, *refs):
    f32, bf16 = jnp.float32, jnp.bfloat16
    ex_n, ey_n, ez_n = dims
    pl_rows = ex_n * ey_n
    n = pl_rows * ez_n
    rest = n - pl_rows
    refs = list(refs)
    (sbr_ref, sbt_ref, tr_ref, tt_ref, xl_ref, xr_ref, yl_ref, yr_ref,
     stiff_ref, lift_ref, inv_ref, field_ref) = refs[:12]
    refs = refs[12:]
    acc_ref = refs.pop(0) if mult is not None else None
    if final:
        top_out, out_ref = refs
    else:
        sel_ref, top_out, acc_out, sb_out, t_out = refs
    sb = jnp.concatenate([sbr_ref[...], sbt_ref[...]], 0)
    t = jnp.concatenate([tr_ref[...], tt_ref[...]], 0)

    def face(f):
        return t[:, f * LANE:(f + 1) * LANE].astype(f32)

    row = lax.broadcasted_iota(jnp.int32, (n, LANE), 0)
    ey = row % ey_n
    parts = []
    xhi, xlo = face(1), face(0)
    pieces = []
    for z in range(ez_n):
        pieces.append(xl_ref[z * ey_n:(z + 1) * ey_n, :].astype(f32))
        pieces.append(xhi[z * pl_rows:(z + 1) * pl_rows - ey_n])
    parts.append((jnp.concatenate(pieces, 0) - xlo).astype(bf16))
    pieces = []
    for z in range(ez_n):
        pieces.append(xlo[z * pl_rows + ey_n:(z + 1) * pl_rows])
        pieces.append(xr_ref[z * ey_n:(z + 1) * ey_n, :].astype(f32))
    parts.append((jnp.concatenate(pieces, 0) - xhi).astype(bf16))
    cols = lax.broadcasted_iota(jnp.int32, (n, n // ey_n), 1)
    rows = lax.broadcasted_iota(jnp.int32, (n, n // ey_n), 0)
    spread = (cols == rows // ey_n).astype(bf16)
    ylo, yhi = face(2), face(3)
    yl = jnp.dot(spread, yl_ref[...], preferred_element_type=f32)
    yr = jnp.dot(spread, yr_ref[...], preferred_element_type=f32)
    nb = jnp.where(ey == 0, yl, pltpu.roll(yhi, 1, 0))
    parts.append((nb - ylo).astype(bf16))
    nb = jnp.where(ey == ey_n - 1, yr, pltpu.roll(ylo, n - 1, 0))
    parts.append((nb - yhi).astype(bf16))
    zlo, zhi = face(4), face(5)
    zero = jnp.zeros((pl_rows, LANE), f32)
    parts.append((jnp.concatenate([zero, zhi[:rest]], 0) - zlo).astype(bf16))
    parts.append((jnp.concatenate([zlo[pl_rows:], zero], 0) - zhi).astype(bf16))
    jumps = jnp.concatenate(parts, -1)
    tot = (jnp.dot(sb, stiff_ref[...], preferred_element_type=f32)
           + jnp.dot(jumps, lift_ref[...], preferred_element_type=f32))
    top_out[...] = tot[rest:]
    k = inv_ref[...] * tot[:rest]
    if mult is None:
        acc = k
    elif mult == 1.0:
        acc = acc_ref[...] + k
    else:
        acc = acc_ref[...] + mult * k
    if final:
        out_ref[...] = field_ref[...] + step_size / 6 * acc
        return
    acc_out[...] = acc
    sbn = (field_ref[...] + coef_next * k).astype(bf16)
    sb_out[...] = sbn
    t_out[...] = jnp.dot(sbn, sel_ref[...], preferred_element_type=f32).astype(bf16)


def top_kernel(coef_next, mult, final, *refs):
    f32, bf16 = jnp.float32, jnp.bfloat16
    refs = list(refs)
    tot_ref, bvals_ref, inv_ref, field_ref = refs[:4]
    refs = refs[4:]
    acc_ref = refs.pop(0) if mult is not None else None
    if final:
        (out_ref,) = refs
    else:
        sel_ref, proj_ref, placet_ref, acc_out, sb_out, t_out, send_out = refs
    k = inv_ref[...] * (tot_ref[...] + bvals_ref[...])
    if mult is None:
        acc = k
    elif mult == 1.0:
        acc = acc_ref[...] + k
    else:
        acc = acc_ref[...] + mult * k
    if final:
        out_ref[...] = field_ref[...] + step_size / 6 * acc
        return
    acc_out[...] = acc
    sbn = (field_ref[...] + coef_next * k).astype(bf16)
    sb_out[...] = sbn
    t = jnp.dot(sbn, sel_ref[...], preferred_element_type=f32).astype(bf16)
    t_out[...] = t
    u = jnp.dot(t[:, 5 * LANE:6 * LANE], proj_ref[...], preferred_element_type=f32).astype(bf16)
    send_out[...] = jnp.dot(placet_ref[...], u, preferred_element_type=f32).astype(bf16)


def exchange(send_u, back_lift, op_blocks, op_columns, place, recv_onehot, devices, capacity, halos):
    f32 = jnp.float32
    recv_u = lax.all_to_all(send_u.reshape(devices, capacity, 64), ("gx", "gy"), 0, 0, tiled=True)
    recv_u = recv_u.reshape(devices * capacity, 64)
    grid = jnp.einsum("rb,rc->bc", recv_onehot, recv_u, preferred_element_type=f32).astype(jnp.bfloat16)
    select = (op_columns[:, :, None] == jnp.arange(NBLK, dtype=jnp.int32)[None, None, :]).astype(jnp.bfloat16)
    gsel = jnp.einsum("ikj,jc->ikc", select, grid, preferred_element_type=f32).astype(jnp.bfloat16)
    w = jnp.einsum("ikc,ikce->ie", gsel, op_blocks, preferred_element_type=f32).astype(jnp.bfloat16)
    reply = jnp.dot(recv_onehot, w, preferred_element_type=f32).astype(jnp.bfloat16)
    reply, halos = lax.optimization_barrier((reply, halos))
    back = lax.all_to_all(reply.reshape(devices, capacity, 64), ("gx", "gy"), 0, 0, tiled=True)
    back = back.reshape(devices * capacity, 64)
    values = jnp.dot(place, back, preferred_element_type=f32).astype(jnp.bfloat16)
    return jnp.dot(values, back_lift, preferred_element_type=f32), halos


def body(field, inv_material, stiffness, lift, projection, back_lift, op_blocks, op_columns, panel_dest, panel_anchor):
    f32, bf16 = jnp.float32, jnp.bfloat16
    ex_n, ey_n, ez_n = field.shape[:3]
    dims = (ex_n, ey_n, ez_n)
    pl_rows = ex_n * ey_n
    n = pl_rows * ez_n
    rest = n - pl_rows
    devices = lax.axis_size("gx") * lax.axis_size("gy")
    panels = ex_n * ey_n
    capacity = max(2, 2 * panels // devices)
    slots = devices * capacity
    dest = panel_dest[:, 0]
    hit = (dest[:, None] == jnp.arange(devices, dtype=jnp.int32)[None, :]).astype(jnp.int32)
    ranks = jnp.cumsum(hit, axis=0)
    slot_of = jnp.sum(hit * (ranks - 1), axis=1)
    position = dest * capacity + slot_of
    place = (position[:, None] == jnp.arange(slots, dtype=jnp.int32)[None, :]).astype(bf16)
    placet = place.T
    code = jnp.einsum("pr,p->r", place, (panel_anchor + 1).astype(bf16), preferred_element_type=f32).astype(bf16)
    recv_code = lax.all_to_all(code.reshape(devices, capacity), ("gx", "gy"), 0, 0, tiled=True)
    recv_code = recv_code.reshape(slots)
    levels = (jnp.arange(NBLK, dtype=jnp.int32) + 1).astype(bf16)
    recv_onehot = (recv_code[:, None] == levels[None, :]).astype(bf16)

    sel = trace_selector()
    lift_pad = pad_faces(lift)
    proj_pad = jnp.concatenate([projection, jnp.zeros((LANE - 96, 64), bf16)], 0)
    ft = field.transpose(2, 0, 1, 3).reshape(n, 384)
    it = inv_material.transpose(2, 0, 1).reshape(n, 1)
    field_r, field_t = ft[:rest], ft[rest:]
    inv_r, inv_t = it[:rest], it[rest:]

    sb_r, sb_t = ft[:rest].astype(bf16), ft[rest:].astype(bf16)
    t_r = jnp.dot(sb_r, sel, preferred_element_type=f32).astype(bf16)
    t_t = jnp.dot(sb_t, sel, preferred_element_type=f32).astype(bf16)
    u = jnp.dot(t_t[:, 5 * LANE:6 * LANE], proj_pad, preferred_element_type=f32).astype(bf16)
    send = jnp.dot(placet, u, preferred_element_type=f32).astype(bf16)
    acc_r = acc_t = None
    coefs = (step_size / 2, step_size / 2, step_size, None)
    mults = (None, 2.0, 2.0, 1.0)
    flops = 2 * n * 384 * (384 + 12 * LANE)
    for i in range(4):
        t4r = t_r.reshape(ez_n - 1, ex_n, ey_n, 6 * LANE)
        t4t = t_t.reshape(1, ex_n, ey_n, 6 * LANE)

        def take(fn):
            return jnp.concatenate([fn(t4r), fn(t4t)], 0)

        x_hi = take(lambda a: a[:, ex_n - 1, :, LANE:2 * LANE]).reshape(ez_n * ey_n, LANE)
        x_lo = take(lambda a: a[:, 0, :, 0:LANE]).reshape(ez_n * ey_n, LANE)
        y_hi = take(lambda a: a[:, :, ey_n - 1, 3 * LANE:4 * LANE]).reshape(ez_n * ex_n, LANE)
        y_lo = take(lambda a: a[:, :, 0, 2 * LANE:3 * LANE]).reshape(ez_n * ex_n, LANE)
        halos = (shift_in(x_hi, "gx", True), shift_in(x_lo, "gx", False),
                 shift_in(y_hi, "gy", True), shift_in(y_lo, "gy", False))
        bvals, halos = exchange(send, back_lift, op_blocks, op_columns, place, recv_onehot, devices, capacity, halos)
        final = i == 3
        ins = [sb_r, sb_t, t_r, t_t, *halos, stiffness, lift_pad, inv_r, field_r]
        if mults[i] is not None:
            ins.append(acc_r)
        kern = functools.partial(rate_kernel, dims, coefs[i], mults[i], final)
        top_shape = jax.ShapeDtypeStruct((pl_rows, 384), f32)
        if final:
            tot_t, out_r = vmem_call(kern, ins, (top_shape, jax.ShapeDtypeStruct((rest, 384), f32)), flops, n * 384 * 16)
        else:
            outs = (top_shape, jax.ShapeDtypeStruct((rest, 384), f32), jax.ShapeDtypeStruct((rest, 384), bf16),
                    jax.ShapeDtypeStruct((rest, 6 * LANE), bf16))
            tot_t, acc_r, sb_r, t_r = vmem_call(kern, ins + [sel], outs, flops, n * 384 * 16)
        ins = [tot_t, bvals, inv_t, field_t]
        if mults[i] is not None:
            ins.append(acc_t)
        kern = functools.partial(top_kernel, coefs[i], mults[i], final)
        if final:
            out_t = vmem_call(kern, ins, jax.ShapeDtypeStruct((pl_rows, 384), f32), 0, pl_rows * 384 * 16)
        else:
            outs = (jax.ShapeDtypeStruct((pl_rows, 384), f32), jax.ShapeDtypeStruct((pl_rows, 384), bf16),
                    jax.ShapeDtypeStruct((pl_rows, 6 * LANE), bf16), jax.ShapeDtypeStruct((slots, 64), bf16))
            acc_t, sb_t, t_t, send = vmem_call(kern, ins + [sel, proj_pad, placet], outs,
                                               2 * pl_rows * 384 * 6 * LANE, pl_rows * 384 * 16)
    out = jnp.concatenate([out_r, out_t], 0).reshape(ez_n, ex_n, ey_n, 384)
    return out.transpose(1, 2, 0, 3)


def solution(mesh):
    return jax.shard_map(
        body,
        mesh=mesh,
        in_specs=(
            P("gx", "gy", None, None),
            P("gx", "gy", None),
            P(), P(), P(), P(), P(), P(),
            P(("gx", "gy"), None),
            P(("gx", "gy")),
        ),
        out_specs=P("gx", "gy", None, None),
        check_vma=False,
    )
```

```python
import functools

import jax
import jax.numpy as jnp
from jax import lax
from jax.experimental import pallas as pl
from jax.experimental.pallas import tpu as pltpu
from jax.sharding import PartitionSpec as P

NBLK = 8
LANE = 128

step_size = 0.25


def shift_in(arr, axis, lower):
    count = lax.axis_size(axis)
    if lower:
        pairs = [(i, i + 1) for i in range(count - 1)]
    else:
        pairs = [(i + 1, i) for i in range(count - 1)]
    return lax.ppermute(arr, axis, pairs)


def trace_selector():
    rows = lax.broadcasted_iota(jnp.int32, (384, 6 * LANE), 0)
    cols = lax.broadcasted_iota(jnp.int32, (384, 6 * LANE), 1)
    face, j = cols // LANE, cols % LANE
    comp, p, q = j // 16, (j // 4) % 4, j % 4
    side = jnp.where(face % 2 == 0, 0, 3)
    ax = face // 2
    a = jnp.where(ax == 0, side, p)
    b = jnp.where(ax == 0, p, jnp.where(ax == 1, side, q))
    c = jnp.where(ax == 2, side, q)
    src = comp * 64 + a * 16 + b * 4 + c
    return ((rows == src) & (j < 96)).astype(jnp.bfloat16)


def pad_faces(mat):
    k = mat.shape[1]
    zero = jnp.zeros((LANE - 96, k), mat.dtype)
    parts = []
    for f in range(6):
        parts += [mat[96 * f:96 * (f + 1)], zero]
    return jnp.concatenate(parts, 0)


def vmem_call(kernel, ins, outs, flops, nbytes):
    vm = pl.BlockSpec(memory_space=pltpu.VMEM)
    multi = isinstance(outs, tuple)
    return pl.pallas_call(
        kernel,
        out_shape=outs,
        in_specs=[vm] * len(ins),
        out_specs=tuple(vm for _ in outs) if multi else vm,
        cost_estimate=pl.CostEstimate(flops=flops, bytes_accessed=nbytes, transcendentals=0),
    )(*ins)


def rate_kernel(dims, coef_next, mult, final, *refs):
    f32, bf16 = jnp.float32, jnp.bfloat16
    ex_n, ey_n, ez_n = dims
    pl_rows = ex_n * ey_n
    n = pl_rows * ez_n
    rest = n - pl_rows
    refs = list(refs)
    (sbr_ref, sbt_ref, tr_ref, tt_ref, xl_ref, xr_ref, yl_ref, yr_ref,
     stiff_ref, lift_ref, inv_ref, field_ref, _) = refs[:13]
    refs = refs[13:]
    acc_ref = refs.pop(0) if mult is not None else None
    if final:
        top_out, out_ref = refs
    else:
        sel_ref, top_out, acc_out, sb_out, t_out = refs
    sb = jnp.concatenate([sbr_ref[...], sbt_ref[...]], 0)
    t = jnp.concatenate([tr_ref[...], tt_ref[...]], 0)

    def face(f):
        return t[:, f * LANE:(f + 1) * LANE].astype(f32)

    row = lax.broadcasted_iota(jnp.int32, (n, LANE), 0)
    ey = row % ey_n
    parts = []
    xhi, xlo = face(1), face(0)
    pieces = []
    for z in range(ez_n):
        pieces.append(xl_ref[z * ey_n:(z + 1) * ey_n, :].astype(f32))
        pieces.append(xhi[z * pl_rows:(z + 1) * pl_rows - ey_n])
    parts.append((jnp.concatenate(pieces, 0) - xlo).astype(bf16))
    pieces = []
    for z in range(ez_n):
        pieces.append(xlo[z * pl_rows + ey_n:(z + 1) * pl_rows])
        pieces.append(xr_ref[z * ey_n:(z + 1) * ey_n, :].astype(f32))
    parts.append((jnp.concatenate(pieces, 0) - xhi).astype(bf16))
    cols = lax.broadcasted_iota(jnp.int32, (n, n // ey_n), 1)
    rows = lax.broadcasted_iota(jnp.int32, (n, n // ey_n), 0)
    spread = (cols == rows // ey_n).astype(bf16)
    ylo, yhi = face(2), face(3)
    yl = jnp.dot(spread, yl_ref[...], preferred_element_type=f32)
    yr = jnp.dot(spread, yr_ref[...], preferred_element_type=f32)
    nb = jnp.where(ey == 0, yl, pltpu.roll(yhi, 1, 0))
    parts.append((nb - ylo).astype(bf16))
    nb = jnp.where(ey == ey_n - 1, yr, pltpu.roll(ylo, n - 1, 0))
    parts.append((nb - yhi).astype(bf16))
    zlo, zhi = face(4), face(5)
    zero = jnp.zeros((pl_rows, LANE), f32)
    parts.append((jnp.concatenate([zero, zhi[:rest]], 0) - zlo).astype(bf16))
    parts.append((jnp.concatenate([zlo[pl_rows:], zero], 0) - zhi).astype(bf16))
    jumps = jnp.concatenate(parts, -1)
    tot = (jnp.dot(sb, stiff_ref[...], preferred_element_type=f32)
           + jnp.dot(jumps, lift_ref[...], preferred_element_type=f32))
    top_out[...] = tot[rest:]
    k = inv_ref[...] * tot[:rest]
    if mult is None:
        acc = k
    elif mult == 1.0:
        acc = acc_ref[...] + k
    else:
        acc = acc_ref[...] + mult * k
    if final:
        out_ref[...] = field_ref[...] + step_size / 6 * acc
        return
    acc_out[...] = acc
    sbn = (field_ref[...] + coef_next * k).astype(bf16)
    sb_out[...] = sbn
    t_out[...] = jnp.dot(sbn, sel_ref[...], preferred_element_type=f32).astype(bf16)


def top_kernel(coef_next, mult, final, *refs):
    f32, bf16 = jnp.float32, jnp.bfloat16
    refs = list(refs)
    tot_ref, bvals_ref, inv_ref, field_ref = refs[:4]
    refs = refs[4:]
    acc_ref = refs.pop(0) if mult is not None else None
    if final:
        (out_ref,) = refs
    else:
        sel_ref, proj_ref, placet_ref, acc_out, sb_out, t_out, send_out = refs
    k = inv_ref[...] * (tot_ref[...] + bvals_ref[...])
    if mult is None:
        acc = k
    elif mult == 1.0:
        acc = acc_ref[...] + k
    else:
        acc = acc_ref[...] + mult * k
    if final:
        out_ref[...] = field_ref[...] + step_size / 6 * acc
        return
    acc_out[...] = acc
    sbn = (field_ref[...] + coef_next * k).astype(bf16)
    sb_out[...] = sbn
    t = jnp.dot(sbn, sel_ref[...], preferred_element_type=f32).astype(bf16)
    t_out[...] = t
    u = jnp.dot(t[:, 5 * LANE:6 * LANE], proj_ref[...], preferred_element_type=f32).astype(bf16)
    send_out[...] = jnp.dot(placet_ref[...], u, preferred_element_type=f32).astype(bf16)


def exchange(send_u, back_lift, op_blocks, op_columns, place, recv_onehot, devices, capacity, halos):
    f32 = jnp.float32
    recv_u = lax.all_to_all(send_u.reshape(devices, capacity, 64), ("gx", "gy"), 0, 0, tiled=True)
    recv_u = recv_u.reshape(devices * capacity, 64)
    grid = jnp.einsum("rb,rc->bc", recv_onehot, recv_u, preferred_element_type=f32).astype(jnp.bfloat16)
    select = (op_columns[:, :, None] == jnp.arange(NBLK, dtype=jnp.int32)[None, None, :]).astype(jnp.bfloat16)
    gsel = jnp.einsum("ikj,jc->ikc", select, grid, preferred_element_type=f32).astype(jnp.bfloat16)
    w = jnp.einsum("ikc,ikce->ie", gsel, op_blocks, preferred_element_type=f32).astype(jnp.bfloat16)
    reply = jnp.dot(recv_onehot, w, preferred_element_type=f32).astype(jnp.bfloat16)
    reply, halos = lax.optimization_barrier((reply, halos))
    back = lax.all_to_all(reply.reshape(devices, capacity, 64), ("gx", "gy"), 0, 0, tiled=True)
    back = back.reshape(devices * capacity, 64)
    values = jnp.dot(place, back, preferred_element_type=f32).astype(jnp.bfloat16)
    return jnp.dot(values, back_lift, preferred_element_type=f32), halos, reply


def body(field, inv_material, stiffness, lift, projection, back_lift, op_blocks, op_columns, panel_dest, panel_anchor):
    f32, bf16 = jnp.float32, jnp.bfloat16
    ex_n, ey_n, ez_n = field.shape[:3]
    dims = (ex_n, ey_n, ez_n)
    pl_rows = ex_n * ey_n
    n = pl_rows * ez_n
    rest = n - pl_rows
    devices = lax.axis_size("gx") * lax.axis_size("gy")
    panels = ex_n * ey_n
    capacity = max(2, 2 * panels // devices)
    slots = devices * capacity
    dest = panel_dest[:, 0]
    hit = (dest[:, None] == jnp.arange(devices, dtype=jnp.int32)[None, :]).astype(jnp.int32)
    ranks = jnp.cumsum(hit, axis=0)
    slot_of = jnp.sum(hit * (ranks - 1), axis=1)
    position = dest * capacity + slot_of
    place = (position[:, None] == jnp.arange(slots, dtype=jnp.int32)[None, :]).astype(bf16)
    placet = place.T
    code = jnp.einsum("pr,p->r", place, (panel_anchor + 1).astype(bf16), preferred_element_type=f32).astype(bf16)
    recv_code = lax.all_to_all(code.reshape(devices, capacity), ("gx", "gy"), 0, 0, tiled=True)
    recv_code = recv_code.reshape(slots)
    levels = (jnp.arange(NBLK, dtype=jnp.int32) + 1).astype(bf16)
    recv_onehot = (recv_code[:, None] == levels[None, :]).astype(bf16)

    sel = trace_selector()
    lift_pad = pad_faces(lift)
    proj_pad = jnp.concatenate([projection, jnp.zeros((LANE - 96, 64), bf16)], 0)
    ft = field.transpose(2, 0, 1, 3).reshape(n, 384)
    it = inv_material.transpose(2, 0, 1).reshape(n, 1)
    field_r, field_t = ft[:rest], ft[rest:]
    inv_r, inv_t = it[:rest], it[rest:]

    sb_r, sb_t = ft[:rest].astype(bf16), ft[rest:].astype(bf16)
    t_r = jnp.dot(sb_r, sel, preferred_element_type=f32).astype(bf16)
    t_t = jnp.dot(sb_t, sel, preferred_element_type=f32).astype(bf16)
    u = jnp.dot(t_t[:, 5 * LANE:6 * LANE], proj_pad, preferred_element_type=f32).astype(bf16)
    send = jnp.dot(placet, u, preferred_element_type=f32).astype(bf16)
    acc_r = acc_t = None
    coefs = (step_size / 2, step_size / 2, step_size, None)
    mults = (None, 2.0, 2.0, 1.0)
    flops = 2 * n * 384 * (384 + 12 * LANE)
    for i in range(4):
        t4r = t_r.reshape(ez_n - 1, ex_n, ey_n, 6 * LANE)
        t4t = t_t.reshape(1, ex_n, ey_n, 6 * LANE)

        def take(fn):
            return jnp.concatenate([fn(t4r), fn(t4t)], 0)

        x_hi = take(lambda a: a[:, ex_n - 1, :, LANE:2 * LANE]).reshape(ez_n * ey_n, LANE)
        x_lo = take(lambda a: a[:, 0, :, 0:LANE]).reshape(ez_n * ey_n, LANE)
        y_hi = take(lambda a: a[:, :, ey_n - 1, 3 * LANE:4 * LANE]).reshape(ez_n * ex_n, LANE)
        y_lo = take(lambda a: a[:, :, 0, 2 * LANE:3 * LANE]).reshape(ez_n * ex_n, LANE)
        halos = (shift_in(x_hi, "gx", True), shift_in(x_lo, "gx", False),
                 shift_in(y_hi, "gy", True), shift_in(y_lo, "gy", False))
        bvals, halos, reply = exchange(send, back_lift, op_blocks, op_columns, place, recv_onehot, devices, capacity, halos)
        final = i == 3
        ins = [sb_r, sb_t, t_r, t_t, *halos, stiffness, lift_pad, inv_r, field_r, reply]
        if mults[i] is not None:
            ins.append(acc_r)
        kern = functools.partial(rate_kernel, dims, coefs[i], mults[i], final)
        top_shape = jax.ShapeDtypeStruct((pl_rows, 384), f32)
        if final:
            tot_t, out_r = vmem_call(kern, ins, (top_shape, jax.ShapeDtypeStruct((rest, 384), f32)), flops, n * 384 * 16)
        else:
            outs = (top_shape, jax.ShapeDtypeStruct((rest, 384), f32), jax.ShapeDtypeStruct((rest, 384), bf16),
                    jax.ShapeDtypeStruct((rest, 6 * LANE), bf16))
            tot_t, acc_r, sb_r, t_r = vmem_call(kern, ins + [sel], outs, flops, n * 384 * 16)
        ins = [tot_t, bvals, inv_t, field_t]
        if mults[i] is not None:
            ins.append(acc_t)
        kern = functools.partial(top_kernel, coefs[i], mults[i], final)
        if final:
            out_t = vmem_call(kern, ins, jax.ShapeDtypeStruct((pl_rows, 384), f32), 0, pl_rows * 384 * 16)
        else:
            outs = (jax.ShapeDtypeStruct((pl_rows, 384), f32), jax.ShapeDtypeStruct((pl_rows, 384), bf16),
                    jax.ShapeDtypeStruct((pl_rows, 6 * LANE), bf16), jax.ShapeDtypeStruct((slots, 64), bf16))
            acc_t, sb_t, t_t, send = vmem_call(kern, ins + [sel, proj_pad, placet], outs,
                                               2 * pl_rows * 384 * 6 * LANE, pl_rows * 384 * 16)
    out = jnp.concatenate([out_r, out_t], 0).reshape(ez_n, ex_n, ey_n, 384)
    return out.transpose(1, 2, 0, 3)


def solution(mesh):
    return jax.shard_map(
        body,
        mesh=mesh,
        in_specs=(
            P("gx", "gy", None, None),
            P("gx", "gy", None),
            P(), P(), P(), P(), P(), P(),
            P(("gx", "gy"), None),
            P(("gx", "gy")),
        ),
        out_specs=P("gx", "gy", None, None),
        check_vma=False,
    )
```

```python
import jax
import jax.numpy as jnp
from jax import lax
from jax.sharding import PartitionSpec as P
from jax.experimental import pallas as pl
from jax.experimental.pallas import tpu as pltpu
import functools

NBLK = 8
LANE = 128

step_size = 0.25


def rate_kernel(ex_n, ey_n, ez_n, sb_ref, t_ref, xl_ref, xr_ref, yl_ref, yr_ref, stiff_ref, lift_ref, out_ref):
    f32, bf16 = jnp.float32, jnp.bfloat16
    n = ex_n * ey_n * ez_n
    plane = ey_n * ez_n
    row = lax.broadcasted_iota(jnp.int32, (n, LANE), 0)
    ez = row % ez_n
    parts = []
    own = t_ref[:, 0:LANE].astype(f32)
    nb = jnp.concatenate([xl_ref[...], t_ref[0:n - plane, LANE:2 * LANE]], 0).astype(f32)
    parts.append((nb - own).astype(bf16))
    own = t_ref[:, LANE:2 * LANE].astype(f32)
    nb = jnp.concatenate([t_ref[plane:n, 0:LANE], xr_ref[...]], 0).astype(f32)
    parts.append((nb - own).astype(bf16))
    own = t_ref[:, 2 * LANE:3 * LANE].astype(f32)
    pieces = []
    for ex in range(ex_n):
        pieces.append(yl_ref[ex * ez_n:(ex + 1) * ez_n, :])
        pieces.append(t_ref[ex * plane:(ex + 1) * plane - ez_n, 3 * LANE:4 * LANE])
    nb = jnp.concatenate(pieces, 0).astype(f32)
    parts.append((nb - own).astype(bf16))
    own = t_ref[:, 3 * LANE:4 * LANE].astype(f32)
    pieces = []
    for ex in range(ex_n):
        pieces.append(t_ref[ex * plane + ez_n:(ex + 1) * plane, 2 * LANE:3 * LANE])
        pieces.append(yr_ref[ex * ez_n:(ex + 1) * ez_n, :])
    nb = jnp.concatenate(pieces, 0).astype(f32)
    parts.append((nb - own).astype(bf16))
    zlo = t_ref[:, 4 * LANE:5 * LANE].astype(f32)
    zhi = t_ref[:, 5 * LANE:6 * LANE].astype(f32)
    nb = jnp.where(ez == 0, 0.0, pltpu.roll(zhi, 1, 0))
    parts.append((nb - zlo).astype(bf16))
    nb = jnp.where(ez == ez_n - 1, 0.0, pltpu.roll(zlo, n - 1, 0))
    parts.append((nb - zhi).astype(bf16))
    jumps = jnp.concatenate(parts, -1)
    out_ref[...] = (jnp.dot(sb_ref[...], stiff_ref[...], preferred_element_type=f32)
                    + jnp.dot(jumps, lift_ref[...], preferred_element_type=f32))


def rate_call(sb, t, xl, xr, yl, yr, stiff, lift_pad, dims):
    ex_n, ey_n, ez_n = dims
    n = ex_n * ey_n * ez_n
    vm = pl.BlockSpec(memory_space=pltpu.VMEM)
    flops = 2 * n * 384 * (384 + 6 * LANE)
    return pl.pallas_call(
        functools.partial(rate_kernel, ex_n, ey_n, ez_n),
        out_shape=jax.ShapeDtypeStruct((n, 384), jnp.float32),
        in_specs=[vm] * 8,
        out_specs=vm,
        cost_estimate=pl.CostEstimate(flops=flops, bytes_accessed=n * (384 * 2 + 768 * 2 + 384 * 4), transcendentals=0),
    )(sb, t, xl, xr, yl, yr, stiff, lift_pad)


def shift_in(arr, axis, dim, lower):
    count = lax.axis_size(axis)
    if lower:
        pairs = [(i, (i + 1) % count) for i in range(count)]
    else:
        pairs = [((i + 1) % count, i) for i in range(count)]
    got = lax.ppermute(arr, axis, pairs)
    edge = 0 if lower else count - 1
    return jnp.where(lax.axis_index(axis) == edge, jnp.zeros_like(got), got)


def trace_selector():
    rows = lax.broadcasted_iota(jnp.int32, (384, 6 * LANE), 0)
    cols = lax.broadcasted_iota(jnp.int32, (384, 6 * LANE), 1)
    face, j = cols // LANE, cols % LANE
    comp, p, q = j // 16, (j // 4) % 4, j % 4
    side = jnp.where(face % 2 == 0, 0, 3)
    ax = face // 2
    a = jnp.where(ax == 0, side, p)
    b = jnp.where(ax == 0, p, jnp.where(ax == 1, side, q))
    c = jnp.where(ax == 2, side, q)
    src = comp * 64 + a * 16 + b * 4 + c
    return ((rows == src) & (j < 96)).astype(jnp.bfloat16)


def pad_faces(mat):
    k = mat.shape[1]
    zero = jnp.zeros((LANE - 96, k), mat.dtype)
    parts = []
    for f in range(6):
        parts += [mat[96 * f:96 * (f + 1)], zero]
    return jnp.concatenate(parts, 0)


def boundary_term(tops, proj_pad, back_lift, op_blocks, op_columns, place, recv_onehot, devices, capacity, halos):
    f32 = jnp.float32
    u = jnp.dot(tops, proj_pad, preferred_element_type=f32).astype(jnp.bfloat16)
    send_u = jnp.einsum("pr,pc->rc", place, u, preferred_element_type=f32).astype(jnp.bfloat16)
    recv_u = lax.all_to_all(send_u.reshape(devices, capacity, 64), ("gx", "gy"), 0, 0, tiled=True)
    recv_u = recv_u.reshape(devices * capacity, 64)
    grid = jnp.einsum("rb,rc->bc", recv_onehot, recv_u, preferred_element_type=f32).astype(jnp.bfloat16)
    select = (op_columns[:, :, None] == jnp.arange(NBLK, dtype=jnp.int32)[None, None, :]).astype(jnp.bfloat16)
    gsel = jnp.einsum("ikj,jc->ikc", select, grid, preferred_element_type=f32).astype(jnp.bfloat16)
    w = jnp.einsum("ikc,ikce->ie", gsel, op_blocks, preferred_element_type=f32).astype(jnp.bfloat16)
    reply = jnp.dot(recv_onehot, w, preferred_element_type=f32).astype(jnp.bfloat16)
    reply, halos = lax.optimization_barrier((reply, halos))
    back = lax.all_to_all(reply.reshape(devices, capacity, 64), ("gx", "gy"), 0, 0, tiled=True)
    back = back.reshape(devices * capacity, 64)
    values = jnp.dot(place, back, preferred_element_type=f32).astype(jnp.bfloat16)
    return jnp.dot(values, back_lift, preferred_element_type=f32), halos


def body(field, inv_material, stiffness, lift, projection, back_lift, op_blocks, op_columns, panel_dest, panel_anchor):
    f32, bf16 = jnp.float32, jnp.bfloat16
    ex_n, ey_n, ez_n = field.shape[:3]
    n = ex_n * ey_n * ez_n
    devices = lax.axis_size("gx") * lax.axis_size("gy")
    panels = ex_n * ey_n
    capacity = max(2, 2 * panels // devices)
    dest = panel_dest[:, 0]
    hit = (dest[:, None] == jnp.arange(devices, dtype=jnp.int32)[None, :]).astype(jnp.int32)
    ranks = jnp.cumsum(hit, axis=0)
    slots = jnp.sum(hit * (ranks - 1), axis=1)
    position = dest * capacity + slots
    place = (position[:, None] == jnp.arange(devices * capacity, dtype=jnp.int32)[None, :]).astype(bf16)
    code = jnp.einsum("pr,p->r", place, (panel_anchor + 1).astype(bf16), preferred_element_type=f32).astype(bf16)
    recv_code = lax.all_to_all(code.reshape(devices, capacity), ("gx", "gy"), 0, 0, tiled=True)
    recv_code = recv_code.reshape(devices * capacity)
    levels = (jnp.arange(NBLK, dtype=jnp.int32) + 1).astype(bf16)
    recv_onehot = (recv_code[:, None] == levels[None, :]).astype(bf16)

    sel = trace_selector()
    lift_pad = pad_faces(lift)
    proj_pad = jnp.concatenate([projection, jnp.zeros((LANE - 96, 64), bf16)], 0)
    inv = inv_material.reshape(n, 1)
    zero_z = jnp.zeros((ex_n, ey_n, 1, LANE), bf16)

    def evaluate(section):
        sb = section.reshape(n, 384).astype(bf16)
        t = jnp.dot(sb, sel, preferred_element_type=f32).astype(bf16)
        t4 = t.reshape(ex_n, ey_n, ez_n, 6 * LANE)
        xlo, xhi = t4[..., 0:LANE], t4[..., LANE:2 * LANE]
        ylo, yhi = t4[..., 2 * LANE:3 * LANE], t4[..., 3 * LANE:4 * LANE]
        zlo, zhi = t4[..., 4 * LANE:5 * LANE], t4[..., 5 * LANE:6 * LANE]
        halo_xl = shift_in(xhi[ex_n - 1:], "gx", 0, True)
        halo_xr = shift_in(xlo[:1], "gx", 0, False)
        halo_yl = shift_in(yhi[:, ey_n - 1:], "gy", 1, True)
        halo_yr = shift_in(ylo[:, :1], "gy", 1, False)
        tops = zhi[:, :, ez_n - 1, :].reshape(panels, LANE)
        bvals, (halo_xl, halo_xr, halo_yl, halo_yr) = boundary_term(
            tops, proj_pad, back_lift, op_blocks, op_columns, place, recv_onehot, devices, capacity,
            (halo_xl, halo_xr, halo_yl, halo_yr))
        total = rate_call(
            sb, t,
            halo_xl.reshape(ey_n * ez_n, LANE), halo_xr.reshape(ey_n * ez_n, LANE),
            halo_yl.reshape(ex_n * ez_n, LANE), halo_yr.reshape(ex_n * ez_n, LANE),
            stiffness, lift_pad, (ex_n, ey_n, ez_n),
        ).reshape(ex_n, ey_n, ez_n, 384)
        top = total[:, :, ez_n - 1:, :] + bvals.reshape(ex_n, ey_n, 1, 384)
        total = jnp.concatenate([total[:, :, :ez_n - 1, :], top], 2)
        return inv_material[..., None] * total

    k_one = evaluate(field)
    k_two = evaluate(field + step_size / 2 * k_one)
    k_three = evaluate(field + step_size / 2 * k_two)
    k_four = evaluate(field + step_size * k_three)
    return field + step_size / 6 * (k_one + 2.0 * k_two + 2.0 * k_three + k_four)


def solution(mesh):
    return jax.shard_map(
        body,
        mesh=mesh,
        in_specs=(
            P("gx", "gy", None, None),
            P("gx", "gy", None),
            P(), P(), P(), P(), P(), P(),
            P(("gx", "gy"), None),
            P(("gx", "gy")),
        ),
        out_specs=P("gx", "gy", None, None),
        check_vma=False,
    )
```

```python
import jax
import jax.numpy as jnp
from jax import lax
from jax.sharding import PartitionSpec as P
from jax.experimental import pallas as pl
from jax.experimental.pallas import tpu as pltpu
import functools

NBLK = 8
LANE = 128

step_size = 0.25


def rate_kernel(ex_n, ey_n, ez_n, sb_ref, t_ref, xl_ref, xr_ref, yl_ref, yr_ref, stiff_ref, lift_ref, out_ref):
    f32, bf16 = jnp.float32, jnp.bfloat16
    n = ex_n * ey_n * ez_n
    plane = ey_n * ez_n
    row = lax.broadcasted_iota(jnp.int32, (n, LANE), 0)
    ez = row % ez_n
    parts = []
    own = t_ref[:, 0:LANE].astype(f32)
    nb = jnp.concatenate([xl_ref[...], t_ref[0:n - plane, LANE:2 * LANE]], 0).astype(f32)
    parts.append((nb - own).astype(bf16))
    own = t_ref[:, LANE:2 * LANE].astype(f32)
    nb = jnp.concatenate([t_ref[plane:n, 0:LANE], xr_ref[...]], 0).astype(f32)
    parts.append((nb - own).astype(bf16))
    own = t_ref[:, 2 * LANE:3 * LANE].astype(f32)
    pieces = []
    for ex in range(ex_n):
        pieces.append(yl_ref[ex * ez_n:(ex + 1) * ez_n, :])
        pieces.append(t_ref[ex * plane:(ex + 1) * plane - ez_n, 3 * LANE:4 * LANE])
    nb = jnp.concatenate(pieces, 0).astype(f32)
    parts.append((nb - own).astype(bf16))
    own = t_ref[:, 3 * LANE:4 * LANE].astype(f32)
    pieces = []
    for ex in range(ex_n):
        pieces.append(t_ref[ex * plane + ez_n:(ex + 1) * plane, 2 * LANE:3 * LANE])
        pieces.append(yr_ref[ex * ez_n:(ex + 1) * ez_n, :])
    nb = jnp.concatenate(pieces, 0).astype(f32)
    parts.append((nb - own).astype(bf16))
    zlo = t_ref[:, 4 * LANE:5 * LANE].astype(f32)
    zhi = t_ref[:, 5 * LANE:6 * LANE].astype(f32)
    nb = jnp.where(ez == 0, 0.0, pltpu.roll(zhi, 1, 0))
    parts.append((nb - zlo).astype(bf16))
    nb = jnp.where(ez == ez_n - 1, 0.0, pltpu.roll(zlo, n - 1, 0))
    parts.append((nb - zhi).astype(bf16))
    jumps = jnp.concatenate(parts, -1)
    out_ref[...] = (jnp.dot(sb_ref[...], stiff_ref[...], preferred_element_type=f32)
                    + jnp.dot(jumps, lift_ref[...], preferred_element_type=f32))


def rate_call(sb, t, xl, xr, yl, yr, stiff, lift_pad, dims):
    ex_n, ey_n, ez_n = dims
    n = ex_n * ey_n * ez_n
    vm = pl.BlockSpec(memory_space=pltpu.VMEM)
    flops = 2 * n * 384 * (384 + 6 * LANE)
    return pl.pallas_call(
        functools.partial(rate_kernel, ex_n, ey_n, ez_n),
        out_shape=jax.ShapeDtypeStruct((n, 384), jnp.float32),
        in_specs=[vm] * 8,
        out_specs=vm,
        cost_estimate=pl.CostEstimate(flops=flops, bytes_accessed=n * (384 * 2 + 768 * 2 + 384 * 4), transcendentals=0),
    )(sb, t, xl, xr, yl, yr, stiff, lift_pad)


def shift_in(arr, axis, dim, lower):
    count = lax.axis_size(axis)
    if lower:
        pairs = [(i, (i + 1) % count) for i in range(count)]
    else:
        pairs = [((i + 1) % count, i) for i in range(count)]
    edge = count - 1 if lower else 0
    arr = jnp.where(lax.axis_index(axis) == edge, jnp.zeros_like(arr), arr)
    return lax.ppermute(arr, axis, pairs)


def trace_selector():
    rows = lax.broadcasted_iota(jnp.int32, (384, 6 * LANE), 0)
    cols = lax.broadcasted_iota(jnp.int32, (384, 6 * LANE), 1)
    face, j = cols // LANE, cols % LANE
    comp, p, q = j // 16, (j // 4) % 4, j % 4
    side = jnp.where(face % 2 == 0, 0, 3)
    ax = face // 2
    a = jnp.where(ax == 0, side, p)
    b = jnp.where(ax == 0, p, jnp.where(ax == 1, side, q))
    c = jnp.where(ax == 2, side, q)
    src = comp * 64 + a * 16 + b * 4 + c
    return ((rows == src) & (j < 96)).astype(jnp.bfloat16)


def pad_faces(mat):
    k = mat.shape[1]
    zero = jnp.zeros((LANE - 96, k), mat.dtype)
    parts = []
    for f in range(6):
        parts += [mat[96 * f:96 * (f + 1)], zero]
    return jnp.concatenate(parts, 0)


def boundary_term(tops, proj_pad, back_lift, op_blocks, op_columns, place, recv_onehot, devices, capacity, halos):
    f32 = jnp.float32
    u = jnp.dot(tops, proj_pad, preferred_element_type=f32).astype(jnp.bfloat16)
    send_u = jnp.einsum("pr,pc->rc", place, u, preferred_element_type=f32).astype(jnp.bfloat16)
    recv_u = lax.all_to_all(send_u.reshape(devices, capacity, 64), ("gx", "gy"), 0, 0, tiled=True)
    recv_u = recv_u.reshape(devices * capacity, 64)
    grid = jnp.einsum("rb,rc->bc", recv_onehot, recv_u, preferred_element_type=f32).astype(jnp.bfloat16)
    select = (op_columns[:, :, None] == jnp.arange(NBLK, dtype=jnp.int32)[None, None, :]).astype(jnp.bfloat16)
    gsel = jnp.einsum("ikj,jc->ikc", select, grid, preferred_element_type=f32).astype(jnp.bfloat16)
    w = jnp.einsum("ikc,ikce->ie", gsel, op_blocks, preferred_element_type=f32).astype(jnp.bfloat16)
    reply = jnp.dot(recv_onehot, w, preferred_element_type=f32).astype(jnp.bfloat16)
    reply, halos = lax.optimization_barrier((reply, halos))
    back = lax.all_to_all(reply.reshape(devices, capacity, 64), ("gx", "gy"), 0, 0, tiled=True)
    back = back.reshape(devices * capacity, 64)
    values = jnp.dot(place, back, preferred_element_type=f32).astype(jnp.bfloat16)
    return jnp.dot(values, back_lift, preferred_element_type=f32), halos


def body(field, inv_material, stiffness, lift, projection, back_lift, op_blocks, op_columns, panel_dest, panel_anchor):
    f32, bf16 = jnp.float32, jnp.bfloat16
    ex_n, ey_n, ez_n = field.shape[:3]
    n = ex_n * ey_n * ez_n
    devices = lax.axis_size("gx") * lax.axis_size("gy")
    panels = ex_n * ey_n
    capacity = max(2, 2 * panels // devices)
    dest = panel_dest[:, 0]
    hit = (dest[:, None] == jnp.arange(devices, dtype=jnp.int32)[None, :]).astype(jnp.int32)
    ranks = jnp.cumsum(hit, axis=0)
    slots = jnp.sum(hit * (ranks - 1), axis=1)
    position = dest * capacity + slots
    place = (position[:, None] == jnp.arange(devices * capacity, dtype=jnp.int32)[None, :]).astype(bf16)
    code = jnp.einsum("pr,p->r", place, (panel_anchor + 1).astype(bf16), preferred_element_type=f32).astype(bf16)
    recv_code = lax.all_to_all(code.reshape(devices, capacity), ("gx", "gy"), 0, 0, tiled=True)
    recv_code = recv_code.reshape(devices * capacity)
    levels = (jnp.arange(NBLK, dtype=jnp.int32) + 1).astype(bf16)
    recv_onehot = (recv_code[:, None] == levels[None, :]).astype(bf16)

    sel = trace_selector()
    lift_pad = pad_faces(lift)
    proj_pad = jnp.concatenate([projection, jnp.zeros((LANE - 96, 64), bf16)], 0)
    inv = inv_material.reshape(n, 1)
    zero_z = jnp.zeros((ex_n, ey_n, 1, LANE), bf16)

    def evaluate(section):
        sb = section.reshape(n, 384).astype(bf16)
        t = jnp.dot(sb, sel, preferred_element_type=f32).astype(bf16)
        t4 = t.reshape(ex_n, ey_n, ez_n, 6 * LANE)
        xlo, xhi = t4[..., 0:LANE], t4[..., LANE:2 * LANE]
        ylo, yhi = t4[..., 2 * LANE:3 * LANE], t4[..., 3 * LANE:4 * LANE]
        zlo, zhi = t4[..., 4 * LANE:5 * LANE], t4[..., 5 * LANE:6 * LANE]
        halo_xl = shift_in(xhi[ex_n - 1:], "gx", 0, True)
        halo_xr = shift_in(xlo[:1], "gx", 0, False)
        halo_yl = shift_in(yhi[:, ey_n - 1:], "gy", 1, True)
        halo_yr = shift_in(ylo[:, :1], "gy", 1, False)
        tops = zhi[:, :, ez_n - 1, :].reshape(panels, LANE)
        bvals, (halo_xl, halo_xr, halo_yl, halo_yr) = boundary_term(
            tops, proj_pad, back_lift, op_blocks, op_columns, place, recv_onehot, devices, capacity,
            (halo_xl, halo_xr, halo_yl, halo_yr))
        total = rate_call(
            sb, t,
            halo_xl.reshape(ey_n * ez_n, LANE), halo_xr.reshape(ey_n * ez_n, LANE),
            halo_yl.reshape(ex_n * ez_n, LANE), halo_yr.reshape(ex_n * ez_n, LANE),
            stiffness, lift_pad, (ex_n, ey_n, ez_n),
        ).reshape(ex_n, ey_n, ez_n, 384)
        top = total[:, :, ez_n - 1:, :] + bvals.reshape(ex_n, ey_n, 1, 384)
        total = jnp.concatenate([total[:, :, :ez_n - 1, :], top], 2)
        return inv_material[..., None] * total

    k_one = evaluate(field)
    k_two = evaluate(field + step_size / 2 * k_one)
    k_three = evaluate(field + step_size / 2 * k_two)
    k_four = evaluate(field + step_size * k_three)
    return field + step_size / 6 * (k_one + 2.0 * k_two + 2.0 * k_three + k_four)


def solution(mesh):
    return jax.shard_map(
        body,
        mesh=mesh,
        in_specs=(
            P("gx", "gy", None, None),
            P("gx", "gy", None),
            P(), P(), P(), P(), P(), P(),
            P(("gx", "gy"), None),
            P(("gx", "gy")),
        ),
        out_specs=P("gx", "gy", None, None),
        check_vma=False,
    )
```

```python
import jax
import jax.numpy as jnp
from jax import lax
from jax.sharding import PartitionSpec as P
from jax.experimental import pallas as pl
from jax.experimental.pallas import tpu as pltpu
import functools

NBLK = 8
LANE = 128

step_size = 0.25


def rate_kernel(ex_n, ey_n, ez_n, sb_ref, t_ref, xl_ref, xr_ref, yl_ref, yr_ref, stiff_ref, lift_ref, flag_ref, out_ref):
    def kept(ref, f):
        v = ref[...]
        return jnp.where(flag_ref[f:f + 1, :] > 0.5, v, jnp.zeros_like(v))

    xl, xr, yl, yr = kept(xl_ref, 0), kept(xr_ref, 1), kept(yl_ref, 2), kept(yr_ref, 3)
    f32, bf16 = jnp.float32, jnp.bfloat16
    n = ex_n * ey_n * ez_n
    plane = ey_n * ez_n
    row = lax.broadcasted_iota(jnp.int32, (n, LANE), 0)
    ez = row % ez_n
    parts = []
    own = t_ref[:, 0:LANE].astype(f32)
    nb = jnp.concatenate([xl, t_ref[0:n - plane, LANE:2 * LANE]], 0).astype(f32)
    parts.append((nb - own).astype(bf16))
    own = t_ref[:, LANE:2 * LANE].astype(f32)
    nb = jnp.concatenate([t_ref[plane:n, 0:LANE], xr], 0).astype(f32)
    parts.append((nb - own).astype(bf16))
    own = t_ref[:, 2 * LANE:3 * LANE].astype(f32)
    pieces = []
    for ex in range(ex_n):
        pieces.append(yl[ex * ez_n:(ex + 1) * ez_n, :])
        pieces.append(t_ref[ex * plane:(ex + 1) * plane - ez_n, 3 * LANE:4 * LANE])
    nb = jnp.concatenate(pieces, 0).astype(f32)
    parts.append((nb - own).astype(bf16))
    own = t_ref[:, 3 * LANE:4 * LANE].astype(f32)
    pieces = []
    for ex in range(ex_n):
        pieces.append(t_ref[ex * plane + ez_n:(ex + 1) * plane, 2 * LANE:3 * LANE])
        pieces.append(yr[ex * ez_n:(ex + 1) * ez_n, :])
    nb = jnp.concatenate(pieces, 0).astype(f32)
    parts.append((nb - own).astype(bf16))
    zlo = t_ref[:, 4 * LANE:5 * LANE].astype(f32)
    zhi = t_ref[:, 5 * LANE:6 * LANE].astype(f32)
    nb = jnp.where(ez == 0, 0.0, pltpu.roll(zhi, 1, 0))
    parts.append((nb - zlo).astype(bf16))
    nb = jnp.where(ez == ez_n - 1, 0.0, pltpu.roll(zlo, n - 1, 0))
    parts.append((nb - zhi).astype(bf16))
    jumps = jnp.concatenate(parts, -1)
    out_ref[...] = (jnp.dot(sb_ref[...], stiff_ref[...], preferred_element_type=f32)
                    + jnp.dot(jumps, lift_ref[...], preferred_element_type=f32))


def rate_call(sb, t, xl, xr, yl, yr, stiff, lift_pad, flags, dims):
    ex_n, ey_n, ez_n = dims
    n = ex_n * ey_n * ez_n
    vm = pl.BlockSpec(memory_space=pltpu.VMEM)
    flops = 2 * n * 384 * (384 + 6 * LANE)
    return pl.pallas_call(
        functools.partial(rate_kernel, ex_n, ey_n, ez_n),
        out_shape=jax.ShapeDtypeStruct((n, 384), jnp.float32),
        in_specs=[vm] * 9,
        out_specs=vm,
        cost_estimate=pl.CostEstimate(flops=flops, bytes_accessed=n * (384 * 2 + 768 * 2 + 384 * 4), transcendentals=0),
    )(sb, t, xl, xr, yl, yr, stiff, lift_pad, flags)


def shift_in(arr, axis, dim, lower):
    count = lax.axis_size(axis)
    if lower:
        pairs = [(i, (i + 1) % count) for i in range(count)]
    else:
        pairs = [((i + 1) % count, i) for i in range(count)]
    return lax.ppermute(arr, axis, pairs)


def halo_flags():
    gx, gy = lax.axis_index("gx"), lax.axis_index("gy")
    valid = jnp.stack([gx != 0, gx != lax.axis_size("gx") - 1, gy != 0, gy != lax.axis_size("gy") - 1,
                       False, False, False, False]).astype(jnp.float32)
    return jnp.broadcast_to(valid[:, None], (8, LANE))


def trace_selector():
    rows = lax.broadcasted_iota(jnp.int32, (384, 6 * LANE), 0)
    cols = lax.broadcasted_iota(jnp.int32, (384, 6 * LANE), 1)
    face, j = cols // LANE, cols % LANE
    comp, p, q = j // 16, (j // 4) % 4, j % 4
    side = jnp.where(face % 2 == 0, 0, 3)
    ax = face // 2
    a = jnp.where(ax == 0, side, p)
    b = jnp.where(ax == 0, p, jnp.where(ax == 1, side, q))
    c = jnp.where(ax == 2, side, q)
    src = comp * 64 + a * 16 + b * 4 + c
    return ((rows == src) & (j < 96)).astype(jnp.bfloat16)


def pad_faces(mat):
    k = mat.shape[1]
    zero = jnp.zeros((LANE - 96, k), mat.dtype)
    parts = []
    for f in range(6):
        parts += [mat[96 * f:96 * (f + 1)], zero]
    return jnp.concatenate(parts, 0)


def boundary_term(tops, proj_pad, back_lift, op_blocks, op_columns, place, recv_onehot, devices, capacity, halos):
    f32 = jnp.float32
    u = jnp.dot(tops, proj_pad, preferred_element_type=f32).astype(jnp.bfloat16)
    send_u = jnp.einsum("pr,pc->rc", place, u, preferred_element_type=f32).astype(jnp.bfloat16)
    recv_u = lax.all_to_all(send_u.reshape(devices, capacity, 64), ("gx", "gy"), 0, 0, tiled=True)
    recv_u = recv_u.reshape(devices * capacity, 64)
    grid = jnp.einsum("rb,rc->bc", recv_onehot, recv_u, preferred_element_type=f32).astype(jnp.bfloat16)
    select = (op_columns[:, :, None] == jnp.arange(NBLK, dtype=jnp.int32)[None, None, :]).astype(jnp.bfloat16)
    gsel = jnp.einsum("ikj,jc->ikc", select, grid, preferred_element_type=f32).astype(jnp.bfloat16)
    w = jnp.einsum("ikc,ikce->ie", gsel, op_blocks, preferred_element_type=f32).astype(jnp.bfloat16)
    reply = jnp.dot(recv_onehot, w, preferred_element_type=f32).astype(jnp.bfloat16)
    reply, halos = lax.optimization_barrier((reply, halos))
    back = lax.all_to_all(reply.reshape(devices, capacity, 64), ("gx", "gy"), 0, 0, tiled=True)
    back = back.reshape(devices * capacity, 64)
    values = jnp.dot(place, back, preferred_element_type=f32).astype(jnp.bfloat16)
    return jnp.dot(values, back_lift, preferred_element_type=f32), halos


def body(field, inv_material, stiffness, lift, projection, back_lift, op_blocks, op_columns, panel_dest, panel_anchor):
    f32, bf16 = jnp.float32, jnp.bfloat16
    ex_n, ey_n, ez_n = field.shape[:3]
    n = ex_n * ey_n * ez_n
    devices = lax.axis_size("gx") * lax.axis_size("gy")
    panels = ex_n * ey_n
    capacity = max(2, 2 * panels // devices)
    dest = panel_dest[:, 0]
    hit = (dest[:, None] == jnp.arange(devices, dtype=jnp.int32)[None, :]).astype(jnp.int32)
    ranks = jnp.cumsum(hit, axis=0)
    slots = jnp.sum(hit * (ranks - 1), axis=1)
    position = dest * capacity + slots
    place = (position[:, None] == jnp.arange(devices * capacity, dtype=jnp.int32)[None, :]).astype(bf16)
    code = jnp.einsum("pr,p->r", place, (panel_anchor + 1).astype(bf16), preferred_element_type=f32).astype(bf16)
    recv_code = lax.all_to_all(code.reshape(devices, capacity), ("gx", "gy"), 0, 0, tiled=True)
    recv_code = recv_code.reshape(devices * capacity)
    levels = (jnp.arange(NBLK, dtype=jnp.int32) + 1).astype(bf16)
    recv_onehot = (recv_code[:, None] == levels[None, :]).astype(bf16)

    sel = trace_selector()
    flags = halo_flags()
    lift_pad = pad_faces(lift)
    proj_pad = jnp.concatenate([projection, jnp.zeros((LANE - 96, 64), bf16)], 0)
    inv = inv_material.reshape(n, 1)
    zero_z = jnp.zeros((ex_n, ey_n, 1, LANE), bf16)

    def evaluate(section):
        sb = section.reshape(n, 384).astype(bf16)
        t = jnp.dot(sb, sel, preferred_element_type=f32).astype(bf16)
        t4 = t.reshape(ex_n, ey_n, ez_n, 6 * LANE)
        xlo, xhi = t4[..., 0:LANE], t4[..., LANE:2 * LANE]
        ylo, yhi = t4[..., 2 * LANE:3 * LANE], t4[..., 3 * LANE:4 * LANE]
        zlo, zhi = t4[..., 4 * LANE:5 * LANE], t4[..., 5 * LANE:6 * LANE]
        halo_xl = shift_in(xhi[ex_n - 1:], "gx", 0, True)
        halo_xr = shift_in(xlo[:1], "gx", 0, False)
        halo_yl = shift_in(yhi[:, ey_n - 1:], "gy", 1, True)
        halo_yr = shift_in(ylo[:, :1], "gy", 1, False)
        tops = zhi[:, :, ez_n - 1, :].reshape(panels, LANE)
        bvals, (halo_xl, halo_xr, halo_yl, halo_yr) = boundary_term(
            tops, proj_pad, back_lift, op_blocks, op_columns, place, recv_onehot, devices, capacity,
            (halo_xl, halo_xr, halo_yl, halo_yr))
        total = rate_call(
            sb, t,
            halo_xl.reshape(ey_n * ez_n, LANE), halo_xr.reshape(ey_n * ez_n, LANE),
            halo_yl.reshape(ex_n * ez_n, LANE), halo_yr.reshape(ex_n * ez_n, LANE),
            stiffness, lift_pad, flags, (ex_n, ey_n, ez_n),
        ).reshape(ex_n, ey_n, ez_n, 384)
        top = total[:, :, ez_n - 1:, :] + bvals.reshape(ex_n, ey_n, 1, 384)
        total = jnp.concatenate([total[:, :, :ez_n - 1, :], top], 2)
        return inv_material[..., None] * total

    k_one = evaluate(field)
    k_two = evaluate(field + step_size / 2 * k_one)
    k_three = evaluate(field + step_size / 2 * k_two)
    k_four = evaluate(field + step_size * k_three)
    return field + step_size / 6 * (k_one + 2.0 * k_two + 2.0 * k_three + k_four)


def solution(mesh):
    return jax.shard_map(
        body,
        mesh=mesh,
        in_specs=(
            P("gx", "gy", None, None),
            P("gx", "gy", None),
            P(), P(), P(), P(), P(), P(),
            P(("gx", "gy"), None),
            P(("gx", "gy")),
        ),
        out_specs=P("gx", "gy", None, None),
        check_vma=False,
    )
```

```python
import jax
import jax.numpy as jnp
from jax import lax
from jax.sharding import PartitionSpec as P
from jax.experimental import pallas as pl
from jax.experimental.pallas import tpu as pltpu
import functools

NBLK = 8
LANE = 128

step_size = 0.25


def rate_kernel(ex_n, ey_n, ez_n, sb_ref, t_ref, xl_ref, xr_ref, yl_ref, yr_ref, stiff_ref, lift_ref, out_ref):
    f32, bf16 = jnp.float32, jnp.bfloat16
    n = ex_n * ey_n * ez_n
    plane = ey_n * ez_n
    row = lax.broadcasted_iota(jnp.int32, (n, LANE), 0)
    ez = row % ez_n
    parts = []
    own = t_ref[:, 0:LANE].astype(f32)
    nb = jnp.concatenate([xl_ref[...], t_ref[0:n - plane, LANE:2 * LANE]], 0).astype(f32)
    parts.append((nb - own).astype(bf16))
    own = t_ref[:, LANE:2 * LANE].astype(f32)
    nb = jnp.concatenate([t_ref[plane:n, 0:LANE], xr_ref[...]], 0).astype(f32)
    parts.append((nb - own).astype(bf16))
    own = t_ref[:, 2 * LANE:3 * LANE].astype(f32)
    pieces = []
    for ex in range(ex_n):
        pieces.append(yl_ref[ex * ez_n:(ex + 1) * ez_n, :])
        pieces.append(t_ref[ex * plane:(ex + 1) * plane - ez_n, 3 * LANE:4 * LANE])
    nb = jnp.concatenate(pieces, 0).astype(f32)
    parts.append((nb - own).astype(bf16))
    own = t_ref[:, 3 * LANE:4 * LANE].astype(f32)
    pieces = []
    for ex in range(ex_n):
        pieces.append(t_ref[ex * plane + ez_n:(ex + 1) * plane, 2 * LANE:3 * LANE])
        pieces.append(yr_ref[ex * ez_n:(ex + 1) * ez_n, :])
    nb = jnp.concatenate(pieces, 0).astype(f32)
    parts.append((nb - own).astype(bf16))
    zlo = t_ref[:, 4 * LANE:5 * LANE].astype(f32)
    zhi = t_ref[:, 5 * LANE:6 * LANE].astype(f32)
    nb = jnp.where(ez == 0, 0.0, pltpu.roll(zhi, 1, 0))
    parts.append((nb - zlo).astype(bf16))
    nb = jnp.where(ez == ez_n - 1, 0.0, pltpu.roll(zlo, n - 1, 0))
    parts.append((nb - zhi).astype(bf16))
    jumps = jnp.concatenate(parts, -1)
    out_ref[...] = (jnp.dot(sb_ref[...], stiff_ref[...], preferred_element_type=f32)
                    + jnp.dot(jumps, lift_ref[...], preferred_element_type=f32))


def rate_call(sb, t, xl, xr, yl, yr, stiff, lift_pad, dims):
    ex_n, ey_n, ez_n = dims
    n = ex_n * ey_n * ez_n
    vm = pl.BlockSpec(memory_space=pltpu.VMEM)
    flops = 2 * n * 384 * (384 + 6 * LANE)
    return pl.pallas_call(
        functools.partial(rate_kernel, ex_n, ey_n, ez_n),
        out_shape=jax.ShapeDtypeStruct((n, 384), jnp.float32),
        in_specs=[vm] * 8,
        out_specs=vm,
        cost_estimate=pl.CostEstimate(flops=flops, bytes_accessed=n * (384 * 2 + 768 * 2 + 384 * 4), transcendentals=0),
    )(sb, t, xl, xr, yl, yr, stiff, lift_pad)


def shift_in(arr, axis, dim, lower):
    count = lax.axis_size(axis)
    if lower:
        pairs = [(i, (i + 1) % count) for i in range(count)]
    else:
        pairs = [((i + 1) % count, i) for i in range(count)]
    got = lax.ppermute(arr, axis, pairs)
    edge = 0 if lower else count - 1
    return jnp.where(lax.axis_index(axis) == edge, jnp.zeros_like(got), got)


def trace_selector():
    rows = lax.broadcasted_iota(jnp.int32, (384, 6 * LANE), 0)
    cols = lax.broadcasted_iota(jnp.int32, (384, 6 * LANE), 1)
    face, j = cols // LANE, cols % LANE
    comp, p, q = j // 16, (j // 4) % 4, j % 4
    side = jnp.where(face % 2 == 0, 0, 3)
    ax = face // 2
    a = jnp.where(ax == 0, side, p)
    b = jnp.where(ax == 0, p, jnp.where(ax == 1, side, q))
    c = jnp.where(ax == 2, side, q)
    src = comp * 64 + a * 16 + b * 4 + c
    return ((rows == src) & (j < 96)).astype(jnp.bfloat16)


def pad_faces(mat):
    k = mat.shape[1]
    zero = jnp.zeros((LANE - 96, k), mat.dtype)
    parts = []
    for f in range(6):
        parts += [mat[96 * f:96 * (f + 1)], zero]
    return jnp.concatenate(parts, 0)

def step_kernel(dims, coef_next, mult, final, *refs):
    f32, bf16 = jnp.float32, jnp.bfloat16
    ex_n, ey_n, ez_n = dims
    refs = list(refs)
    sb_ref, t_ref, xl_ref, xr_ref, yl_ref, yr_ref, stiff_ref, lift_ref, bvals_ref, inv_ref, field_ref = refs[:11]
    refs = refs[11:]
    acc_ref = refs.pop(0) if mult is not None else None
    if final:
        (out_ref,) = refs
    else:
        sel_ref, seltop_ref, proj_ref, placet_ref, acc_out, sb_out, t_out, send_out = refs
    n = ex_n * ey_n * ez_n
    plane = ey_n * ez_n
    row = lax.broadcasted_iota(jnp.int32, (n, LANE), 0)
    ez = row % ez_n
    parts = []
    own = t_ref[:, 0:LANE].astype(f32)
    nb = jnp.concatenate([xl_ref[...], t_ref[0:n - plane, LANE:2 * LANE]], 0).astype(f32)
    parts.append((nb - own).astype(bf16))
    own = t_ref[:, LANE:2 * LANE].astype(f32)
    nb = jnp.concatenate([t_ref[plane:n, 0:LANE], xr_ref[...]], 0).astype(f32)
    parts.append((nb - own).astype(bf16))
    own = t_ref[:, 2 * LANE:3 * LANE].astype(f32)
    pieces = []
    for ex in range(ex_n):
        pieces.append(yl_ref[ex * ez_n:(ex + 1) * ez_n, :])
        pieces.append(t_ref[ex * plane:(ex + 1) * plane - ez_n, 3 * LANE:4 * LANE])
    nb = jnp.concatenate(pieces, 0).astype(f32)
    parts.append((nb - own).astype(bf16))
    own = t_ref[:, 3 * LANE:4 * LANE].astype(f32)
    pieces = []
    for ex in range(ex_n):
        pieces.append(t_ref[ex * plane + ez_n:(ex + 1) * plane, 2 * LANE:3 * LANE])
        pieces.append(yr_ref[ex * ez_n:(ex + 1) * ez_n, :])
    nb = jnp.concatenate(pieces, 0).astype(f32)
    parts.append((nb - own).astype(bf16))
    zlo = t_ref[:, 4 * LANE:5 * LANE].astype(f32)
    zhi = t_ref[:, 5 * LANE:6 * LANE].astype(f32)
    nb = jnp.where(ez == 0, 0.0, pltpu.roll(zhi, 1, 0))
    parts.append((nb - zlo).astype(bf16))
    nb = jnp.where(ez == ez_n - 1, 0.0, pltpu.roll(zlo, n - 1, 0))
    parts.append((nb - zhi).astype(bf16))
    jumps = jnp.concatenate(parts, -1)
    tot = (jnp.dot(sb_ref[...], stiff_ref[...], preferred_element_type=f32)
           + jnp.dot(jumps, lift_ref[...], preferred_element_type=f32))
    width = tot.shape[1]
    tot = tot.reshape(n // ez_n, ez_n, width)
    top = lax.broadcasted_iota(jnp.int32, tot.shape, 1) == ez_n - 1
    tot = jnp.where(top, tot + bvals_ref[...][:, None, :], tot).reshape(n, width)
    k = inv_ref[...] * tot
    if mult is None:
        acc = k
    elif mult == 1.0:
        acc = acc_ref[...] + k
    else:
        acc = acc_ref[...] + mult * k
    if final:
        out_ref[...] = field_ref[...] + step_size / 6 * acc
        return
    acc_out[...] = acc
    sb = (field_ref[...] + coef_next * k).astype(bf16)
    sb_out[...] = sb
    t = jnp.dot(sb, sel_ref[...], preferred_element_type=f32).astype(bf16)
    t_out[...] = t
    tops = jnp.dot(seltop_ref[...], t[:, 5 * LANE:6 * LANE], preferred_element_type=f32).astype(bf16)
    u = jnp.dot(tops, proj_ref[...], preferred_element_type=f32).astype(bf16)
    send_out[...] = jnp.dot(placet_ref[...], u, preferred_element_type=f32).astype(bf16)


def step_call(ins, dims, coef_next, mult, final, slots):
    n = dims[0] * dims[1] * dims[2]
    vm = pl.BlockSpec(memory_space=pltpu.VMEM)
    if final:
        outs = jax.ShapeDtypeStruct((n, 384), jnp.float32)
        out_specs = vm
    else:
        outs = (jax.ShapeDtypeStruct((n, 384), jnp.float32), jax.ShapeDtypeStruct((n, 384), jnp.bfloat16),
                jax.ShapeDtypeStruct((n, 6 * LANE), jnp.bfloat16), jax.ShapeDtypeStruct((slots, 64), jnp.bfloat16))
        out_specs = (vm, vm, vm, vm)
    flops = 2 * n * 384 * (384 + 12 * LANE)
    return pl.pallas_call(
        functools.partial(step_kernel, dims, coef_next, mult, final),
        out_shape=outs,
        in_specs=[vm] * len(ins),
        out_specs=out_specs,
        cost_estimate=pl.CostEstimate(flops=flops, bytes_accessed=n * 384 * 4 * 6, transcendentals=0),
    )(*ins)


def exchange(send_u, back_lift, op_blocks, op_columns, place, recv_onehot, devices, capacity, halos):
    f32 = jnp.float32
    recv_u = lax.all_to_all(send_u.reshape(devices, capacity, 64), ("gx", "gy"), 0, 0, tiled=True)
    recv_u = recv_u.reshape(devices * capacity, 64)
    grid = jnp.einsum("rb,rc->bc", recv_onehot, recv_u, preferred_element_type=f32).astype(jnp.bfloat16)
    select = (op_columns[:, :, None] == jnp.arange(NBLK, dtype=jnp.int32)[None, None, :]).astype(jnp.bfloat16)
    gsel = jnp.einsum("ikj,jc->ikc", select, grid, preferred_element_type=f32).astype(jnp.bfloat16)
    w = jnp.einsum("ikc,ikce->ie", gsel, op_blocks, preferred_element_type=f32).astype(jnp.bfloat16)
    reply = jnp.dot(recv_onehot, w, preferred_element_type=f32).astype(jnp.bfloat16)
    reply, halos = lax.optimization_barrier((reply, halos))
    back = lax.all_to_all(reply.reshape(devices, capacity, 64), ("gx", "gy"), 0, 0, tiled=True)
    back = back.reshape(devices * capacity, 64)
    values = jnp.dot(place, back, preferred_element_type=f32).astype(jnp.bfloat16)
    return jnp.dot(values, back_lift, preferred_element_type=f32), halos


def body(field, inv_material, stiffness, lift, projection, back_lift, op_blocks, op_columns, panel_dest, panel_anchor):
    f32, bf16 = jnp.float32, jnp.bfloat16
    ex_n, ey_n, ez_n = field.shape[:3]
    n = ex_n * ey_n * ez_n
    devices = lax.axis_size("gx") * lax.axis_size("gy")
    panels = ex_n * ey_n
    capacity = max(2, 2 * panels // devices)
    dest = panel_dest[:, 0]
    hit = (dest[:, None] == jnp.arange(devices, dtype=jnp.int32)[None, :]).astype(jnp.int32)
    ranks = jnp.cumsum(hit, axis=0)
    slots = jnp.sum(hit * (ranks - 1), axis=1)
    position = dest * capacity + slots
    place = (position[:, None] == jnp.arange(devices * capacity, dtype=jnp.int32)[None, :]).astype(bf16)
    code = jnp.einsum("pr,p->r", place, (panel_anchor + 1).astype(bf16), preferred_element_type=f32).astype(bf16)
    recv_code = lax.all_to_all(code.reshape(devices, capacity), ("gx", "gy"), 0, 0, tiled=True)
    recv_code = recv_code.reshape(devices * capacity)
    levels = (jnp.arange(NBLK, dtype=jnp.int32) + 1).astype(bf16)
    recv_onehot = (recv_code[:, None] == levels[None, :]).astype(bf16)

    sel = trace_selector()
    lift_pad = pad_faces(lift)
    proj_pad = jnp.concatenate([projection, jnp.zeros((LANE - 96, 64), bf16)], 0)
    inv = inv_material.reshape(n, 1)
    zero_z = jnp.zeros((ex_n, ey_n, 1, LANE), bf16)

    fieldf = field.reshape(n, 384)
    inv = inv_material.reshape(n, 1)
    placet = place.T
    rows = lax.broadcasted_iota(jnp.int32, (panels, n), 1)
    seltop = (rows == lax.broadcasted_iota(jnp.int32, (panels, n), 0) * ez_n + ez_n - 1).astype(bf16)
    dims = (ex_n, ey_n, ez_n)

    sb = fieldf.astype(bf16)
    t = jnp.dot(sb, sel, preferred_element_type=f32).astype(bf16)
    tops = t.reshape(ex_n, ey_n, ez_n, 6 * LANE)[:, :, ez_n - 1, 5 * LANE:6 * LANE].reshape(panels, LANE)
    u = jnp.dot(tops, proj_pad, preferred_element_type=f32).astype(bf16)
    send = jnp.dot(placet, u, preferred_element_type=f32).astype(bf16)
    acc = None
    coefs = (step_size / 2, step_size / 2, step_size, None)
    mults = (None, 2.0, 2.0, 1.0)
    for i in range(4):
        t4 = t.reshape(ex_n, ey_n, ez_n, 6 * LANE)
        xlo, xhi = t4[..., 0:LANE], t4[..., LANE:2 * LANE]
        ylo, yhi = t4[..., 2 * LANE:3 * LANE], t4[..., 3 * LANE:4 * LANE]
        halos = (
            shift_in(xhi[ex_n - 1:], "gx", 0, True).reshape(ey_n * ez_n, LANE),
            shift_in(xlo[:1], "gx", 0, False).reshape(ey_n * ez_n, LANE),
            shift_in(yhi[:, ey_n - 1:], "gy", 1, True).reshape(ex_n * ez_n, LANE),
            shift_in(ylo[:, :1], "gy", 1, False).reshape(ex_n * ez_n, LANE),
        )
        bvals, halos = exchange(send, back_lift, op_blocks, op_columns, place, recv_onehot, devices, capacity, halos)
        final = i == 3
        ins = [sb, t, *halos, stiffness, lift_pad, bvals, inv, fieldf]
        if mults[i] is not None:
            ins.append(acc)
        if final:
            out = step_call(ins, dims, coefs[i], mults[i], True, devices * capacity)
        else:
            ins += [sel, seltop, proj_pad, placet]
            acc, sb, t, send = step_call(ins, dims, coefs[i], mults[i], False, devices * capacity)
    return out.reshape(field.shape)


def solution(mesh):
    return jax.shard_map(
        body,
        mesh=mesh,
        in_specs=(
            P("gx", "gy", None, None),
            P("gx", "gy", None),
            P(), P(), P(), P(), P(), P(),
            P(("gx", "gy"), None),
            P(("gx", "gy")),
        ),
        out_specs=P("gx", "gy", None, None),
        check_vma=False,
    )
```

```python
import jax
import jax.numpy as jnp
from jax import lax
from jax.sharding import PartitionSpec as P
from jax.experimental import pallas as pl
from jax.experimental.pallas import tpu as pltpu
import functools

NBLK = 8
LANE = 128

step_size = 0.25


def rate_kernel(ex_n, ey_n, ez_n, sb_ref, t_ref, xl_ref, xr_ref, yl_ref, yr_ref, stiff_ref, lift_ref, out_ref):
    f32, bf16 = jnp.float32, jnp.bfloat16
    n = ex_n * ey_n * ez_n
    plane = ey_n * ez_n
    row = lax.broadcasted_iota(jnp.int32, (n, LANE), 0)
    ez = row % ez_n
    parts = []
    own = t_ref[:, 0:LANE].astype(f32)
    nb = jnp.concatenate([xl_ref[...], t_ref[0:n - plane, LANE:2 * LANE]], 0).astype(f32)
    parts.append((nb - own).astype(bf16))
    own = t_ref[:, LANE:2 * LANE].astype(f32)
    nb = jnp.concatenate([t_ref[plane:n, 0:LANE], xr_ref[...]], 0).astype(f32)
    parts.append((nb - own).astype(bf16))
    own = t_ref[:, 2 * LANE:3 * LANE].astype(f32)
    pieces = []
    for ex in range(ex_n):
        pieces.append(yl_ref[ex * ez_n:(ex + 1) * ez_n, :])
        pieces.append(t_ref[ex * plane:(ex + 1) * plane - ez_n, 3 * LANE:4 * LANE])
    nb = jnp.concatenate(pieces, 0).astype(f32)
    parts.append((nb - own).astype(bf16))
    own = t_ref[:, 3 * LANE:4 * LANE].astype(f32)
    pieces = []
    for ex in range(ex_n):
        pieces.append(t_ref[ex * plane + ez_n:(ex + 1) * plane, 2 * LANE:3 * LANE])
        pieces.append(yr_ref[ex * ez_n:(ex + 1) * ez_n, :])
    nb = jnp.concatenate(pieces, 0).astype(f32)
    parts.append((nb - own).astype(bf16))
    zlo = t_ref[:, 4 * LANE:5 * LANE].astype(f32)
    zhi = t_ref[:, 5 * LANE:6 * LANE].astype(f32)
    nb = jnp.where(ez == 0, 0.0, pltpu.roll(zhi, 1, 0))
    parts.append((nb - zlo).astype(bf16))
    nb = jnp.where(ez == ez_n - 1, 0.0, pltpu.roll(zlo, n - 1, 0))
    parts.append((nb - zhi).astype(bf16))
    jumps = jnp.concatenate(parts, -1)
    out_ref[...] = (jnp.dot(sb_ref[...], stiff_ref[...], preferred_element_type=f32)
                    + jnp.dot(jumps, lift_ref[...], preferred_element_type=f32))


def rate_call(sb, t, xl, xr, yl, yr, stiff, lift_pad, dims):
    ex_n, ey_n, ez_n = dims
    n = ex_n * ey_n * ez_n
    vm = pl.BlockSpec(memory_space=pltpu.VMEM)
    flops = 2 * n * 384 * (384 + 6 * LANE)
    return pl.pallas_call(
        functools.partial(rate_kernel, ex_n, ey_n, ez_n),
        out_shape=jax.ShapeDtypeStruct((n, 384), jnp.float32),
        in_specs=[vm] * 8,
        out_specs=vm,
        cost_estimate=pl.CostEstimate(flops=flops, bytes_accessed=n * (384 * 2 + 768 * 2 + 384 * 4), transcendentals=0),
    )(sb, t, xl, xr, yl, yr, stiff, lift_pad)


def shift_in(arr, axis, dim, lower):
    count = lax.axis_size(axis)
    if lower:
        pairs = [(i, (i + 1) % count) for i in range(count)]
    else:
        pairs = [((i + 1) % count, i) for i in range(count)]
    got = lax.ppermute(arr, axis, pairs)
    edge = 0 if lower else count - 1
    return jnp.where(lax.axis_index(axis) == edge, jnp.zeros_like(got), got)


def trace_selector():
    rows = lax.broadcasted_iota(jnp.int32, (384, 6 * LANE), 0)
    cols = lax.broadcasted_iota(jnp.int32, (384, 6 * LANE), 1)
    face, j = cols // LANE, cols % LANE
    comp, p, q = j // 16, (j // 4) % 4, j % 4
    side = jnp.where(face % 2 == 0, 0, 3)
    ax = face // 2
    a = jnp.where(ax == 0, side, p)
    b = jnp.where(ax == 0, p, jnp.where(ax == 1, side, q))
    c = jnp.where(ax == 2, side, q)
    src = comp * 64 + a * 16 + b * 4 + c
    return ((rows == src) & (j < 96)).astype(jnp.bfloat16)


def pad_faces(mat):
    k = mat.shape[1]
    zero = jnp.zeros((LANE - 96, k), mat.dtype)
    parts = []
    for f in range(6):
        parts += [mat[96 * f:96 * (f + 1)], zero]
    return jnp.concatenate(parts, 0)


def boundary_term(tops, proj_pad, back_lift, op_blocks, op_columns, place, recv_onehot, devices, capacity, section, prepare):
    f32 = jnp.float32
    u = jnp.dot(tops, proj_pad, preferred_element_type=f32).astype(jnp.bfloat16)
    send_u = jnp.einsum("pr,pc->rc", place, u, preferred_element_type=f32).astype(jnp.bfloat16)
    recv_u = lax.all_to_all(send_u.reshape(devices, capacity, 64), ("gx", "gy"), 0, 0, tiled=True)
    recv_u = recv_u.reshape(devices * capacity, 64)
    recv_u, section = lax.optimization_barrier((recv_u, section))
    sb, t, halos = prepare(section)
    grid = jnp.einsum("rb,rc->bc", recv_onehot, recv_u, preferred_element_type=f32).astype(jnp.bfloat16)
    select = (op_columns[:, :, None] == jnp.arange(NBLK, dtype=jnp.int32)[None, None, :]).astype(jnp.bfloat16)
    gsel = jnp.einsum("ikj,jc->ikc", select, grid, preferred_element_type=f32).astype(jnp.bfloat16)
    w = jnp.einsum("ikc,ikce->ie", gsel, op_blocks, preferred_element_type=f32).astype(jnp.bfloat16)
    reply = jnp.dot(recv_onehot, w, preferred_element_type=f32).astype(jnp.bfloat16)
    reply, halos = lax.optimization_barrier((reply, halos))
    back = lax.all_to_all(reply.reshape(devices, capacity, 64), ("gx", "gy"), 0, 0, tiled=True)
    back = back.reshape(devices * capacity, 64)
    values = jnp.dot(place, back, preferred_element_type=f32).astype(jnp.bfloat16)
    return jnp.dot(values, back_lift, preferred_element_type=f32), sb, t, halos


def body(field, inv_material, stiffness, lift, projection, back_lift, op_blocks, op_columns, panel_dest, panel_anchor):
    f32, bf16 = jnp.float32, jnp.bfloat16
    ex_n, ey_n, ez_n = field.shape[:3]
    n = ex_n * ey_n * ez_n
    devices = lax.axis_size("gx") * lax.axis_size("gy")
    panels = ex_n * ey_n
    capacity = max(2, 2 * panels // devices)
    dest = panel_dest[:, 0]
    hit = (dest[:, None] == jnp.arange(devices, dtype=jnp.int32)[None, :]).astype(jnp.int32)
    ranks = jnp.cumsum(hit, axis=0)
    slots = jnp.sum(hit * (ranks - 1), axis=1)
    position = dest * capacity + slots
    place = (position[:, None] == jnp.arange(devices * capacity, dtype=jnp.int32)[None, :]).astype(bf16)
    code = jnp.einsum("pr,p->r", place, (panel_anchor + 1).astype(bf16), preferred_element_type=f32).astype(bf16)
    recv_code = lax.all_to_all(code.reshape(devices, capacity), ("gx", "gy"), 0, 0, tiled=True)
    recv_code = recv_code.reshape(devices * capacity)
    levels = (jnp.arange(NBLK, dtype=jnp.int32) + 1).astype(bf16)
    recv_onehot = (recv_code[:, None] == levels[None, :]).astype(bf16)

    sel = trace_selector()
    lift_pad = pad_faces(lift)
    proj_pad = jnp.concatenate([projection, jnp.zeros((LANE - 96, 64), bf16)], 0)
    inv = inv_material.reshape(n, 1)
    zero_z = jnp.zeros((ex_n, ey_n, 1, LANE), bf16)

    def prepare(section):
        sb = section.reshape(n, 384).astype(bf16)
        t = jnp.dot(sb, sel, preferred_element_type=f32).astype(bf16)
        t4 = t.reshape(ex_n, ey_n, ez_n, 6 * LANE)
        xlo, xhi = t4[..., 0:LANE], t4[..., LANE:2 * LANE]
        ylo, yhi = t4[..., 2 * LANE:3 * LANE], t4[..., 3 * LANE:4 * LANE]
        halos = (shift_in(xhi[ex_n - 1:], "gx", 0, True), shift_in(xlo[:1], "gx", 0, False),
                 shift_in(yhi[:, ey_n - 1:], "gy", 1, True), shift_in(ylo[:, :1], "gy", 1, False))
        return sb, t, halos

    def evaluate(section, tops):
        bvals, sb, t, (halo_xl, halo_xr, halo_yl, halo_yr) = boundary_term(
            tops, proj_pad, back_lift, op_blocks, op_columns, place, recv_onehot, devices, capacity,
            section, prepare)
        total = rate_call(
            sb, t,
            halo_xl.reshape(ey_n * ez_n, LANE), halo_xr.reshape(ey_n * ez_n, LANE),
            halo_yl.reshape(ex_n * ez_n, LANE), halo_yr.reshape(ex_n * ez_n, LANE),
            stiffness, lift_pad, (ex_n, ey_n, ez_n),
        ).reshape(ex_n, ey_n, ez_n, 384)
        top = total[:, :, ez_n - 1, :] + bvals.reshape(ex_n, ey_n, 384)
        total = jnp.concatenate([total[:, :, :ez_n - 1, :], top[:, :, None, :]], 2)
        return inv_material[..., None] * total, inv_material[:, :, ez_n - 1, None] * top

    sel_top = sel[:, 5 * LANE:6 * LANE]

    def tops_of(section_top):
        sbt = section_top.reshape(panels, 384).astype(bf16)
        return jnp.dot(sbt, sel_top, preferred_element_type=f32).astype(bf16)

    field_top = field[:, :, ez_n - 1, :]
    k_one, top_one = evaluate(field, tops_of(field_top))
    k_two, top_two = evaluate(field + step_size / 2 * k_one, tops_of(field_top + step_size / 2 * top_one))
    k_three, top_three = evaluate(field + step_size / 2 * k_two, tops_of(field_top + step_size / 2 * top_two))
    k_four, _ = evaluate(field + step_size * k_three, tops_of(field_top + step_size * top_three))
    return field + step_size / 6 * (k_one + 2.0 * k_two + 2.0 * k_three + k_four)


def solution(mesh):
    return jax.shard_map(
        body,
        mesh=mesh,
        in_specs=(
            P("gx", "gy", None, None),
            P("gx", "gy", None),
            P(), P(), P(), P(), P(), P(),
            P(("gx", "gy"), None),
            P(("gx", "gy")),
        ),
        out_specs=P("gx", "gy", None, None),
        check_vma=False,
    )
```

```python
import jax
import jax.numpy as jnp
from jax import lax
from jax.sharding import PartitionSpec as P
from jax.experimental import pallas as pl
from jax.experimental.pallas import tpu as pltpu
import functools

NBLK = 8
LANE = 128

step_size = 0.25


def rate_kernel(ex_n, ey_n, ez_n, sb_ref, t_ref, xl_ref, xr_ref, yl_ref, yr_ref, stiff_ref, lift_ref, out_ref):
    f32, bf16 = jnp.float32, jnp.bfloat16
    n = ex_n * ey_n * ez_n
    plane = ey_n * ez_n
    row = lax.broadcasted_iota(jnp.int32, (n, LANE), 0)
    ez = row % ez_n
    parts = []
    own = t_ref[:, 0:LANE].astype(f32)
    nb = jnp.concatenate([xl_ref[...], t_ref[0:n - plane, LANE:2 * LANE]], 0).astype(f32)
    parts.append((nb - own).astype(bf16))
    own = t_ref[:, LANE:2 * LANE].astype(f32)
    nb = jnp.concatenate([t_ref[plane:n, 0:LANE], xr_ref[...]], 0).astype(f32)
    parts.append((nb - own).astype(bf16))
    own = t_ref[:, 2 * LANE:3 * LANE].astype(f32)
    pieces = []
    for ex in range(ex_n):
        pieces.append(yl_ref[ex * ez_n:(ex + 1) * ez_n, :])
        pieces.append(t_ref[ex * plane:(ex + 1) * plane - ez_n, 3 * LANE:4 * LANE])
    nb = jnp.concatenate(pieces, 0).astype(f32)
    parts.append((nb - own).astype(bf16))
    own = t_ref[:, 3 * LANE:4 * LANE].astype(f32)
    pieces = []
    for ex in range(ex_n):
        pieces.append(t_ref[ex * plane + ez_n:(ex + 1) * plane, 2 * LANE:3 * LANE])
        pieces.append(yr_ref[ex * ez_n:(ex + 1) * ez_n, :])
    nb = jnp.concatenate(pieces, 0).astype(f32)
    parts.append((nb - own).astype(bf16))
    zlo = t_ref[:, 4 * LANE:5 * LANE].astype(f32)
    zhi = t_ref[:, 5 * LANE:6 * LANE].astype(f32)
    nb = jnp.where(ez == 0, 0.0, pltpu.roll(zhi, 1, 0))
    parts.append((nb - zlo).astype(bf16))
    nb = jnp.where(ez == ez_n - 1, 0.0, pltpu.roll(zlo, n - 1, 0))
    parts.append((nb - zhi).astype(bf16))
    jumps = jnp.concatenate(parts, -1)
    out_ref[...] = (jnp.dot(sb_ref[...], stiff_ref[...], preferred_element_type=f32)
                    + jnp.dot(jumps, lift_ref[...], preferred_element_type=f32))


def rate_call(sb, t, xl, xr, yl, yr, stiff, lift_pad, dims):
    ex_n, ey_n, ez_n = dims
    n = ex_n * ey_n * ez_n
    vm = pl.BlockSpec(memory_space=pltpu.VMEM)
    flops = 2 * n * 384 * (384 + 6 * LANE)
    return pl.pallas_call(
        functools.partial(rate_kernel, ex_n, ey_n, ez_n),
        out_shape=jax.ShapeDtypeStruct((n, 384), jnp.float32),
        in_specs=[vm] * 8,
        out_specs=vm,
        cost_estimate=pl.CostEstimate(flops=flops, bytes_accessed=n * (384 * 2 + 768 * 2 + 384 * 4), transcendentals=0),
    )(sb, t, xl, xr, yl, yr, stiff, lift_pad)


def shift_in(arr, axis, dim, lower):
    count = lax.axis_size(axis)
    if lower:
        pairs = [(i, (i + 1) % count) for i in range(count)]
    else:
        pairs = [((i + 1) % count, i) for i in range(count)]
    got = lax.ppermute(arr, axis, pairs)
    edge = 0 if lower else count - 1
    return jnp.where(lax.axis_index(axis) == edge, jnp.zeros_like(got), got)


def trace_selector():
    rows = lax.broadcasted_iota(jnp.int32, (384, 6 * LANE), 0)
    cols = lax.broadcasted_iota(jnp.int32, (384, 6 * LANE), 1)
    face, j = cols // LANE, cols % LANE
    comp, p, q = j // 16, (j // 4) % 4, j % 4
    side = jnp.where(face % 2 == 0, 0, 3)
    ax = face // 2
    a = jnp.where(ax == 0, side, p)
    b = jnp.where(ax == 0, p, jnp.where(ax == 1, side, q))
    c = jnp.where(ax == 2, side, q)
    src = comp * 64 + a * 16 + b * 4 + c
    return ((rows == src) & (j < 96)).astype(jnp.bfloat16)


def pad_faces(mat):
    k = mat.shape[1]
    zero = jnp.zeros((LANE - 96, k), mat.dtype)
    parts = []
    for f in range(6):
        parts += [mat[96 * f:96 * (f + 1)], zero]
    return jnp.concatenate(parts, 0)


def boundary_term(tops, proj_pad, back_lift, op_blocks, op_columns, place, recv_onehot, devices, capacity, halos):
    f32 = jnp.float32
    u = jnp.dot(tops, proj_pad, preferred_element_type=f32).astype(jnp.bfloat16)
    send_u = jnp.einsum("pr,pc->rc", place, u, preferred_element_type=f32).astype(jnp.bfloat16)
    recv_u = lax.all_to_all(send_u.reshape(devices, capacity, 64), ("gx", "gy"), 0, 0, tiled=True)
    recv_u = recv_u.reshape(devices * capacity, 64)
    grid = jnp.einsum("rb,rc->bc", recv_onehot, recv_u, preferred_element_type=f32).astype(jnp.bfloat16)
    select = (op_columns[:, :, None] == jnp.arange(NBLK, dtype=jnp.int32)[None, None, :]).astype(jnp.bfloat16)
    gsel = jnp.einsum("ikj,jc->ikc", select, grid, preferred_element_type=f32).astype(jnp.bfloat16)
    w = jnp.einsum("ikc,ikce->ie", gsel, op_blocks, preferred_element_type=f32).astype(jnp.bfloat16)
    reply = jnp.dot(recv_onehot, w, preferred_element_type=f32).astype(jnp.bfloat16)
    reply, halos = lax.optimization_barrier((reply, halos))
    back = lax.all_to_all(reply.reshape(devices, capacity, 64), ("gx", "gy"), 0, 0, tiled=True)
    back = back.reshape(devices * capacity, 64)
    values = jnp.dot(place, back, preferred_element_type=f32).astype(jnp.bfloat16)
    return jnp.dot(values, back_lift, preferred_element_type=f32), halos


def body(field, inv_material, stiffness, lift, projection, back_lift, op_blocks, op_columns, panel_dest, panel_anchor):
    f32, bf16 = jnp.float32, jnp.bfloat16
    ex_n, ey_n, ez_n = field.shape[:3]
    n = ex_n * ey_n * ez_n
    devices = lax.axis_size("gx") * lax.axis_size("gy")
    panels = ex_n * ey_n
    capacity = max(2, 2 * panels // devices)
    dest = panel_dest[:, 0]
    hit = (dest[:, None] == jnp.arange(devices, dtype=jnp.int32)[None, :]).astype(jnp.int32)
    ranks = jnp.cumsum(hit, axis=0)
    slots = jnp.sum(hit * (ranks - 1), axis=1)
    position = dest * capacity + slots
    place = (position[:, None] == jnp.arange(devices * capacity, dtype=jnp.int32)[None, :]).astype(bf16)
    code = jnp.einsum("pr,p->r", place, (panel_anchor + 1).astype(bf16), preferred_element_type=f32).astype(bf16)
    recv_code = lax.all_to_all(code.reshape(devices, capacity), ("gx", "gy"), 0, 0, tiled=True)
    recv_code = recv_code.reshape(devices * capacity)
    levels = (jnp.arange(NBLK, dtype=jnp.int32) + 1).astype(bf16)
    recv_onehot = (recv_code[:, None] == levels[None, :]).astype(bf16)

    sel = trace_selector()
    lift_pad = pad_faces(lift)
    proj_pad = jnp.concatenate([projection, jnp.zeros((LANE - 96, 64), bf16)], 0)
    inv = inv_material.reshape(n, 1)
    zero_z = jnp.zeros((ex_n, ey_n, 1, LANE), bf16)

    def evaluate(section):
        sb = section.reshape(n, 384).astype(bf16)
        t = jnp.dot(sb, sel, preferred_element_type=f32).astype(bf16)
        t4 = t.reshape(ex_n, ey_n, ez_n, 6 * LANE)
        xlo, xhi = t4[..., 0:LANE], t4[..., LANE:2 * LANE]
        ylo, yhi = t4[..., 2 * LANE:3 * LANE], t4[..., 3 * LANE:4 * LANE]
        zlo, zhi = t4[..., 4 * LANE:5 * LANE], t4[..., 5 * LANE:6 * LANE]
        halo_xl = shift_in(xhi[ex_n - 1:], "gx", 0, True)
        halo_xr = shift_in(xlo[:1], "gx", 0, False)
        halo_yl = shift_in(yhi[:, ey_n - 1:], "gy", 1, True)
        halo_yr = shift_in(ylo[:, :1], "gy", 1, False)
        tops = zhi[:, :, ez_n - 1, :].reshape(panels, LANE)
        bvals, (halo_xl, halo_xr, halo_yl, halo_yr) = boundary_term(
            tops, proj_pad, back_lift, op_blocks, op_columns, place, recv_onehot, devices, capacity,
            (halo_xl, halo_xr, halo_yl, halo_yr))
        total = rate_call(
            sb, t,
            halo_xl.reshape(ey_n * ez_n, LANE), halo_xr.reshape(ey_n * ez_n, LANE),
            halo_yl.reshape(ex_n * ez_n, LANE), halo_yr.reshape(ex_n * ez_n, LANE),
            stiffness, lift_pad, (ex_n, ey_n, ez_n),
        ).reshape(ex_n, ey_n, ez_n, 384)
        top = total[:, :, ez_n - 1:, :] + bvals.reshape(ex_n, ey_n, 1, 384)
        total = jnp.concatenate([total[:, :, :ez_n - 1, :], top], 2)
        return inv_material[..., None] * total

    k_one = evaluate(field)
    k_two = evaluate(field + step_size / 2 * k_one)
    acc, section = lax.optimization_barrier((k_one + 2.0 * k_two, field + step_size / 2 * k_two))
    k_three = evaluate(section)
    acc, section = lax.optimization_barrier((acc + 2.0 * k_three, field + step_size * k_three))
    k_four = evaluate(section)
    return field + step_size / 6 * (acc + k_four)


def solution(mesh):
    return jax.shard_map(
        body,
        mesh=mesh,
        in_specs=(
            P("gx", "gy", None, None),
            P("gx", "gy", None),
            P(), P(), P(), P(), P(), P(),
            P(("gx", "gy"), None),
            P(("gx", "gy")),
        ),
        out_specs=P("gx", "gy", None, None),
        check_vma=False,
    )
```

```python
import jax
import jax.numpy as jnp
from jax import lax
from jax.sharding import PartitionSpec as P
from jax.experimental import pallas as pl
from jax.experimental.pallas import tpu as pltpu
import functools

NBLK = 8
LANE = 128

step_size = 0.25


def rate_kernel(ex_n, ey_n, ez_n, sb_ref, t_ref, xl_ref, xr_ref, yl_ref, yr_ref, stiff_ref, lift_ref, out_ref):
    f32, bf16 = jnp.float32, jnp.bfloat16
    n = ex_n * ey_n * ez_n
    plane = ey_n * ez_n
    row = lax.broadcasted_iota(jnp.int32, (n, LANE), 0)
    ez = row % ez_n
    parts = []
    own = t_ref[:, 0:LANE].astype(f32)
    nb = jnp.concatenate([xl_ref[...], t_ref[0:n - plane, LANE:2 * LANE]], 0).astype(f32)
    parts.append((nb - own).astype(bf16))
    own = t_ref[:, LANE:2 * LANE].astype(f32)
    nb = jnp.concatenate([t_ref[plane:n, 0:LANE], xr_ref[...]], 0).astype(f32)
    parts.append((nb - own).astype(bf16))
    own = t_ref[:, 2 * LANE:3 * LANE].astype(f32)
    pieces = []
    for ex in range(ex_n):
        pieces.append(yl_ref[ex * ez_n:(ex + 1) * ez_n, :])
        pieces.append(t_ref[ex * plane:(ex + 1) * plane - ez_n, 3 * LANE:4 * LANE])
    nb = jnp.concatenate(pieces, 0).astype(f32)
    parts.append((nb - own).astype(bf16))
    own = t_ref[:, 3 * LANE:4 * LANE].astype(f32)
    pieces = []
    for ex in range(ex_n):
        pieces.append(t_ref[ex * plane + ez_n:(ex + 1) * plane, 2 * LANE:3 * LANE])
        pieces.append(yr_ref[ex * ez_n:(ex + 1) * ez_n, :])
    nb = jnp.concatenate(pieces, 0).astype(f32)
    parts.append((nb - own).astype(bf16))
    zlo = t_ref[:, 4 * LANE:5 * LANE].astype(f32)
    zhi = t_ref[:, 5 * LANE:6 * LANE].astype(f32)
    nb = jnp.where(ez == 0, 0.0, pltpu.roll(zhi, 1, 0))
    parts.append((nb - zlo).astype(bf16))
    nb = jnp.where(ez == ez_n - 1, 0.0, pltpu.roll(zlo, n - 1, 0))
    parts.append((nb - zhi).astype(bf16))
    jumps = jnp.concatenate(parts, -1)
    out_ref[...] = (jnp.dot(sb_ref[...], stiff_ref[...], preferred_element_type=f32)
                    + jnp.dot(jumps, lift_ref[...], preferred_element_type=f32))


def rate_call(sb, t, xl, xr, yl, yr, stiff, lift_pad, dims):
    ex_n, ey_n, ez_n = dims
    n = ex_n * ey_n * ez_n
    vm = pl.BlockSpec(memory_space=pltpu.VMEM)
    flops = 2 * n * 384 * (384 + 6 * LANE)
    return pl.pallas_call(
        functools.partial(rate_kernel, ex_n, ey_n, ez_n),
        out_shape=jax.ShapeDtypeStruct((n, 384), jnp.float32),
        in_specs=[vm] * 8,
        out_specs=vm,
        cost_estimate=pl.CostEstimate(flops=flops, bytes_accessed=n * (384 * 2 + 768 * 2 + 384 * 4), transcendentals=0),
    )(sb, t, xl, xr, yl, yr, stiff, lift_pad)


def shift_in(arr, axis, dim, lower):
    count = lax.axis_size(axis)
    if lower:
        pairs = [(i, (i + 1) % count) for i in range(count)]
    else:
        pairs = [((i + 1) % count, i) for i in range(count)]
    got = lax.ppermute(arr, axis, pairs)
    edge = 0 if lower else count - 1
    return jnp.where(lax.axis_index(axis) == edge, jnp.zeros_like(got), got)


def trace_selector():
    rows = lax.broadcasted_iota(jnp.int32, (384, 6 * LANE), 0)
    cols = lax.broadcasted_iota(jnp.int32, (384, 6 * LANE), 1)
    face, j = cols // LANE, cols % LANE
    comp, p, q = j // 16, (j // 4) % 4, j % 4
    side = jnp.where(face % 2 == 0, 0, 3)
    ax = face // 2
    a = jnp.where(ax == 0, side, p)
    b = jnp.where(ax == 0, p, jnp.where(ax == 1, side, q))
    c = jnp.where(ax == 2, side, q)
    src = comp * 64 + a * 16 + b * 4 + c
    return ((rows == src) & (j < 96)).astype(jnp.bfloat16)


def pad_faces(mat):
    k = mat.shape[1]
    zero = jnp.zeros((LANE - 96, k), mat.dtype)
    parts = []
    for f in range(6):
        parts += [mat[96 * f:96 * (f + 1)], zero]
    return jnp.concatenate(parts, 0)


def boundary_term(tops, proj_pad, back_lift, op_blocks, op_columns, place, recv_onehot, devices, capacity, halos):
    f32 = jnp.float32
    u = jnp.dot(tops, proj_pad, preferred_element_type=f32).astype(jnp.bfloat16)
    send_u = jnp.einsum("pr,pc->rc", place, u, preferred_element_type=f32).astype(jnp.bfloat16)
    recv_u = lax.all_to_all(send_u.reshape(devices, capacity, 64), ("gx", "gy"), 0, 0, tiled=True)
    recv_u = recv_u.reshape(devices * capacity, 64)
    grid = jnp.einsum("rb,rc->bc", recv_onehot, recv_u, preferred_element_type=f32).astype(jnp.bfloat16)
    select = (op_columns[:, :, None] == jnp.arange(NBLK, dtype=jnp.int32)[None, None, :]).astype(jnp.bfloat16)
    gsel = jnp.einsum("ikj,jc->ikc", select, grid, preferred_element_type=f32).astype(jnp.bfloat16)
    w = jnp.einsum("ikc,ikce->ie", gsel, op_blocks, preferred_element_type=f32).astype(jnp.bfloat16)
    reply = jnp.dot(recv_onehot, w, preferred_element_type=f32).astype(jnp.bfloat16)
    reply, halos = lax.optimization_barrier((reply, halos))
    back = lax.all_to_all(reply.reshape(devices, capacity, 64), ("gx", "gy"), 0, 0, tiled=True)
    back = back.reshape(devices * capacity, 64)
    values = jnp.dot(place, back, preferred_element_type=f32).astype(jnp.bfloat16)
    return jnp.dot(values, back_lift, preferred_element_type=f32), halos


def body(field, inv_material, stiffness, lift, projection, back_lift, op_blocks, op_columns, panel_dest, panel_anchor):
    f32, bf16 = jnp.float32, jnp.bfloat16
    ex_n, ey_n, ez_n = field.shape[:3]
    n = ex_n * ey_n * ez_n
    devices = lax.axis_size("gx") * lax.axis_size("gy")
    panels = ex_n * ey_n
    capacity = max(2, 2 * panels // devices)
    dest = panel_dest[:, 0]
    hit = (dest[:, None] == jnp.arange(devices, dtype=jnp.int32)[None, :]).astype(jnp.int32)
    ranks = jnp.cumsum(hit, axis=0)
    slots = jnp.sum(hit * (ranks - 1), axis=1)
    position = dest * capacity + slots
    place = (position[:, None] == jnp.arange(devices * capacity, dtype=jnp.int32)[None, :]).astype(bf16)
    code = jnp.einsum("pr,p->r", place, (panel_anchor + 1).astype(bf16), preferred_element_type=f32).astype(bf16)
    recv_code = lax.all_to_all(code.reshape(devices, capacity), ("gx", "gy"), 0, 0, tiled=True)
    recv_code = recv_code.reshape(devices * capacity)
    levels = (jnp.arange(NBLK, dtype=jnp.int32) + 1).astype(bf16)
    recv_onehot = (recv_code[:, None] == levels[None, :]).astype(bf16)

    sel = trace_selector()
    lift_pad = pad_faces(lift)
    proj_pad = jnp.concatenate([projection, jnp.zeros((LANE - 96, 64), bf16)], 0)
    inv = inv_material.reshape(n, 1)
    zero_z = jnp.zeros((ex_n, ey_n, 1, LANE), bf16)

    def evaluate(section):
        sb = section.reshape(n, 384).astype(bf16)
        t = jnp.dot(sb, sel, preferred_element_type=f32).astype(bf16)
        t4 = t.reshape(ex_n, ey_n, ez_n, 6 * LANE)
        xlo, xhi = t4[..., 0:LANE], t4[..., LANE:2 * LANE]
        ylo, yhi = t4[..., 2 * LANE:3 * LANE], t4[..., 3 * LANE:4 * LANE]
        zlo, zhi = t4[..., 4 * LANE:5 * LANE], t4[..., 5 * LANE:6 * LANE]
        halo_xl = shift_in(xhi[ex_n - 1:], "gx", 0, True)
        halo_xr = shift_in(xlo[:1], "gx", 0, False)
        t3 = t.reshape(ex_n, ey_n * ez_n, 6 * LANE)
        halo_yl = shift_in(t3[:, (ey_n - 1) * ez_n:, 3 * LANE:4 * LANE], "gy", 1, True)
        halo_yr = shift_in(t3[:, :ez_n, 2 * LANE:3 * LANE], "gy", 1, False)
        tops = zhi[:, :, ez_n - 1, :].reshape(panels, LANE)
        bvals, (halo_xl, halo_xr, halo_yl, halo_yr) = boundary_term(
            tops, proj_pad, back_lift, op_blocks, op_columns, place, recv_onehot, devices, capacity,
            (halo_xl, halo_xr, halo_yl, halo_yr))
        total = rate_call(
            sb, t,
            halo_xl.reshape(ey_n * ez_n, LANE), halo_xr.reshape(ey_n * ez_n, LANE),
            halo_yl.reshape(ex_n * ez_n, LANE), halo_yr.reshape(ex_n * ez_n, LANE),
            stiffness, lift_pad, (ex_n, ey_n, ez_n),
        ).reshape(ex_n, ey_n, ez_n, 384)
        top = total[:, :, ez_n - 1:, :] + bvals.reshape(ex_n, ey_n, 1, 384)
        total = jnp.concatenate([total[:, :, :ez_n - 1, :], top], 2)
        return inv_material[..., None] * total

    k_one = evaluate(field)
    k_two = evaluate(field + step_size / 2 * k_one)
    k_three = evaluate(field + step_size / 2 * k_two)
    k_four = evaluate(field + step_size * k_three)
    return field + step_size / 6 * (k_one + 2.0 * k_two + 2.0 * k_three + k_four)


def solution(mesh):
    return jax.shard_map(
        body,
        mesh=mesh,
        in_specs=(
            P("gx", "gy", None, None),
            P("gx", "gy", None),
            P(), P(), P(), P(), P(), P(),
            P(("gx", "gy"), None),
            P(("gx", "gy")),
        ),
        out_specs=P("gx", "gy", None, None),
        check_vma=False,
    )
```

```python
import jax
import jax.numpy as jnp
from jax import lax
from jax.sharding import PartitionSpec as P
from jax.experimental import pallas as pl
from jax.experimental.pallas import tpu as pltpu
import functools

NBLK = 8
LANE = 128

step_size = 0.25


def rate_kernel(ex_n, ey_n, ez_n, sb_ref, t_ref, xl_ref, xr_ref, yl_ref, yr_ref, stiff_ref, lift_ref, out_ref):
    f32, bf16 = jnp.float32, jnp.bfloat16
    n = ex_n * ey_n * ez_n
    plane = ey_n * ez_n
    row = lax.broadcasted_iota(jnp.int32, (n, LANE), 0)
    ez = row % ez_n
    parts = []
    own = t_ref[:, 0:LANE].astype(f32)
    nb = jnp.concatenate([xl_ref[...], t_ref[0:n - plane, LANE:2 * LANE]], 0).astype(f32)
    parts.append((nb - own).astype(bf16))
    own = t_ref[:, LANE:2 * LANE].astype(f32)
    nb = jnp.concatenate([t_ref[plane:n, 0:LANE], xr_ref[...]], 0).astype(f32)
    parts.append((nb - own).astype(bf16))
    own = t_ref[:, 2 * LANE:3 * LANE].astype(f32)
    pieces = []
    for ex in range(ex_n):
        pieces.append(yl_ref[ex * ez_n:(ex + 1) * ez_n, :])
        pieces.append(t_ref[ex * plane:(ex + 1) * plane - ez_n, 3 * LANE:4 * LANE])
    nb = jnp.concatenate(pieces, 0).astype(f32)
    parts.append((nb - own).astype(bf16))
    own = t_ref[:, 3 * LANE:4 * LANE].astype(f32)
    pieces = []
    for ex in range(ex_n):
        pieces.append(t_ref[ex * plane + ez_n:(ex + 1) * plane, 2 * LANE:3 * LANE])
        pieces.append(yr_ref[ex * ez_n:(ex + 1) * ez_n, :])
    nb = jnp.concatenate(pieces, 0).astype(f32)
    parts.append((nb - own).astype(bf16))
    zlo = t_ref[:, 4 * LANE:5 * LANE].astype(f32)
    zhi = t_ref[:, 5 * LANE:6 * LANE].astype(f32)
    nb = jnp.where(ez == 0, 0.0, pltpu.roll(zhi, 1, 0))
    parts.append((nb - zlo).astype(bf16))
    nb = jnp.where(ez == ez_n - 1, 0.0, pltpu.roll(zlo, n - 1, 0))
    parts.append((nb - zhi).astype(bf16))
    jumps = jnp.concatenate(parts, -1)
    out_ref[...] = (jnp.dot(sb_ref[...], stiff_ref[...], preferred_element_type=f32)
                    + jnp.dot(jumps, lift_ref[...], preferred_element_type=f32))


def rate_call(sb, t, xl, xr, yl, yr, stiff, lift_pad, dims):
    ex_n, ey_n, ez_n = dims
    n = ex_n * ey_n * ez_n
    vm = pl.BlockSpec(memory_space=pltpu.VMEM)
    flops = 2 * n * 384 * (384 + 6 * LANE)
    return pl.pallas_call(
        functools.partial(rate_kernel, ex_n, ey_n, ez_n),
        out_shape=jax.ShapeDtypeStruct((n, 384), jnp.float32),
        in_specs=[vm] * 8,
        out_specs=vm,
        cost_estimate=pl.CostEstimate(flops=flops, bytes_accessed=n * (384 * 2 + 768 * 2 + 384 * 4), transcendentals=0),
    )(sb, t, xl, xr, yl, yr, stiff, lift_pad)


def shift_in(arr, axis, dim, lower):
    count = lax.axis_size(axis)
    if lower:
        pairs = [(i, (i + 1) % count) for i in range(count)]
    else:
        pairs = [((i + 1) % count, i) for i in range(count)]
    got = lax.ppermute(arr, axis, pairs)
    edge = 0 if lower else count - 1
    return jnp.where(lax.axis_index(axis) == edge, jnp.zeros_like(got), got)


def trace_selector():
    rows = lax.broadcasted_iota(jnp.int32, (384, 6 * LANE), 0)
    cols = lax.broadcasted_iota(jnp.int32, (384, 6 * LANE), 1)
    face, j = cols // LANE, cols % LANE
    comp, p, q = j // 16, (j // 4) % 4, j % 4
    side = jnp.where(face % 2 == 0, 0, 3)
    ax = face // 2
    a = jnp.where(ax == 0, side, p)
    b = jnp.where(ax == 0, p, jnp.where(ax == 1, side, q))
    c = jnp.where(ax == 2, side, q)
    src = comp * 64 + a * 16 + b * 4 + c
    return ((rows == src) & (j < 96)).astype(jnp.bfloat16)


def pad_faces(mat):
    k = mat.shape[1]
    zero = jnp.zeros((LANE - 96, k), mat.dtype)
    parts = []
    for f in range(6):
        parts += [mat[96 * f:96 * (f + 1)], zero]
    return jnp.concatenate(parts, 0)


def boundary_term(tops, proj_pad, back_lift, op_blocks, op_columns, place, recv_onehot, devices, capacity, halos, code=None):
    f32 = jnp.float32
    u = jnp.dot(tops, proj_pad, preferred_element_type=f32).astype(jnp.bfloat16)
    send_u = jnp.einsum("pr,pc->rc", place, u, preferred_element_type=f32).astype(jnp.bfloat16)
    if code is None:
        recv_u = lax.all_to_all(send_u.reshape(devices, capacity, 64), ("gx", "gy"), 0, 0, tiled=True)
        recv_u = recv_u.reshape(devices * capacity, 64)
    else:
        pad = jnp.zeros((devices * capacity, 63), jnp.bfloat16)
        both = jnp.concatenate([send_u, code[:, None], pad], 1)
        both = lax.all_to_all(both.reshape(devices, capacity, 128), ("gx", "gy"), 0, 0, tiled=True)
        both = both.reshape(devices * capacity, 128)
        recv_u = both[:, :64]
        levels = (jnp.arange(NBLK, dtype=jnp.int32) + 1).astype(jnp.bfloat16)
        recv_onehot = (both[:, 64:65] == levels[None, :]).astype(jnp.bfloat16)
    grid = jnp.einsum("rb,rc->bc", recv_onehot, recv_u, preferred_element_type=f32).astype(jnp.bfloat16)
    select = (op_columns[:, :, None] == jnp.arange(NBLK, dtype=jnp.int32)[None, None, :]).astype(jnp.bfloat16)
    gsel = jnp.einsum("ikj,jc->ikc", select, grid, preferred_element_type=f32).astype(jnp.bfloat16)
    w = jnp.einsum("ikc,ikce->ie", gsel, op_blocks, preferred_element_type=f32).astype(jnp.bfloat16)
    reply = jnp.dot(recv_onehot, w, preferred_element_type=f32).astype(jnp.bfloat16)
    reply, halos = lax.optimization_barrier((reply, halos))
    back = lax.all_to_all(reply.reshape(devices, capacity, 64), ("gx", "gy"), 0, 0, tiled=True)
    back = back.reshape(devices * capacity, 64)
    values = jnp.dot(place, back, preferred_element_type=f32).astype(jnp.bfloat16)
    return jnp.dot(values, back_lift, preferred_element_type=f32), halos, recv_onehot


def body(field, inv_material, stiffness, lift, projection, back_lift, op_blocks, op_columns, panel_dest, panel_anchor):
    f32, bf16 = jnp.float32, jnp.bfloat16
    ex_n, ey_n, ez_n = field.shape[:3]
    n = ex_n * ey_n * ez_n
    devices = lax.axis_size("gx") * lax.axis_size("gy")
    panels = ex_n * ey_n
    capacity = max(2, 2 * panels // devices)
    dest = panel_dest[:, 0]
    hit = (dest[:, None] == jnp.arange(devices, dtype=jnp.int32)[None, :]).astype(jnp.int32)
    ranks = jnp.cumsum(hit, axis=0)
    slots = jnp.sum(hit * (ranks - 1), axis=1)
    position = dest * capacity + slots
    place = (position[:, None] == jnp.arange(devices * capacity, dtype=jnp.int32)[None, :]).astype(bf16)
    code = jnp.einsum("pr,p->r", place, (panel_anchor + 1).astype(bf16), preferred_element_type=f32).astype(bf16)

    sel = trace_selector()
    lift_pad = pad_faces(lift)
    proj_pad = jnp.concatenate([projection, jnp.zeros((LANE - 96, 64), bf16)], 0)
    inv = inv_material.reshape(n, 1)
    zero_z = jnp.zeros((ex_n, ey_n, 1, LANE), bf16)

    def evaluate(section, recv_onehot, code=None):
        sb = section.reshape(n, 384).astype(bf16)
        t = jnp.dot(sb, sel, preferred_element_type=f32).astype(bf16)
        t4 = t.reshape(ex_n, ey_n, ez_n, 6 * LANE)
        xlo, xhi = t4[..., 0:LANE], t4[..., LANE:2 * LANE]
        ylo, yhi = t4[..., 2 * LANE:3 * LANE], t4[..., 3 * LANE:4 * LANE]
        zlo, zhi = t4[..., 4 * LANE:5 * LANE], t4[..., 5 * LANE:6 * LANE]
        halo_xl = shift_in(xhi[ex_n - 1:], "gx", 0, True)
        halo_xr = shift_in(xlo[:1], "gx", 0, False)
        t3 = t.reshape(ex_n, ey_n * ez_n, 6 * LANE)
        halo_yl = shift_in(t3[:, (ey_n - 1) * ez_n:, 3 * LANE:4 * LANE], "gy", 1, True)
        halo_yr = shift_in(t3[:, :ez_n, 2 * LANE:3 * LANE], "gy", 1, False)
        tops = zhi[:, :, ez_n - 1, :].reshape(panels, LANE)
        bvals, (halo_xl, halo_xr, halo_yl, halo_yr), recv_onehot = boundary_term(
            tops, proj_pad, back_lift, op_blocks, op_columns, place, recv_onehot, devices, capacity,
            (halo_xl, halo_xr, halo_yl, halo_yr), code)
        total = rate_call(
            sb, t,
            halo_xl.reshape(ey_n * ez_n, LANE), halo_xr.reshape(ey_n * ez_n, LANE),
            halo_yl.reshape(ex_n * ez_n, LANE), halo_yr.reshape(ex_n * ez_n, LANE),
            stiffness, lift_pad, (ex_n, ey_n, ez_n),
        ).reshape(ex_n, ey_n, ez_n, 384)
        top = total[:, :, ez_n - 1:, :] + bvals.reshape(ex_n, ey_n, 1, 384)
        total = jnp.concatenate([total[:, :, :ez_n - 1, :], top], 2)
        return inv_material[..., None] * total, recv_onehot

    k_one, recv_onehot = evaluate(field, None, code)
    k_two, _ = evaluate(field + step_size / 2 * k_one, recv_onehot)
    k_three, _ = evaluate(field + step_size / 2 * k_two, recv_onehot)
    k_four, _ = evaluate(field + step_size * k_three, recv_onehot)
    return field + step_size / 6 * (k_one + 2.0 * k_two + 2.0 * k_three + k_four)


def solution(mesh):
    return jax.shard_map(
        body,
        mesh=mesh,
        in_specs=(
            P("gx", "gy", None, None),
            P("gx", "gy", None),
            P(), P(), P(), P(), P(), P(),
            P(("gx", "gy"), None),
            P(("gx", "gy")),
        ),
        out_specs=P("gx", "gy", None, None),
        check_vma=False,
    )
```
